512 devices in a mesh: dp: 32 (over y, x_lo, core), expert: 16 (over x_hi, z).
Axes of the slice: x: 4 (x_hi: 2, x_lo: 2; x = x_hi * 2 + x_lo), y: 8, z: 8, core: 2. Of those that a mesh axis runs over, the one named last changes fastest.
Arguments:
- tokens: bfloat16 [65536, 1024], P(('dp', 'expert')), may hold values from -24 to 24
- routing: int32 [65536, 2], P(('dp', 'expert')), may hold values from 0 to 15, as said below
- combine: float32 [65536, 2], P(('dp', 'expert')), may hold values from 0.1 to 1
- upstream: bfloat16 [65536, 1024], P(('dp', 'expert')), may hold values from -6 to 6
- gate_weight: bfloat16 [16, 1024, 384], P('expert', 'dp'), may hold values from -0.1875 to 0.1875
- up_weight: bfloat16 [16, 1024, 384], P('expert', 'dp'), may hold values from -0.1875 to 0.1875
- down_weight: bfloat16 [16, 1024, 384], P('expert', 'dp'), may hold values from -0.3125 to 0.3125
Outputs:
- layer_output: bfloat16 [65536, 1024], P(('dp', 'expert'))
- token_grad: bfloat16 [65536, 1024], P(('dp', 'expert'))
- combine_grad: float32 [65536, 2], P(('dp', 'expert'))
- gate_grad: float32 [16, 1024, 384], P('expert', 'dp')
- up_grad: float32 [16, 1024, 384], P('expert', 'dp')
The draws below stay inside these ranges and needn't reach their ends.
Inputs may be any that keep to these rules, and one draw needn't show every extreme that they name: `routing`: each row names 2 different experts. The rows fall into blocks of 128 (the rows of one device), and 16 consecutive blocks form a data group. In each data group one expert, the group's hot expert, is named by exactly 64 rows of every block of the group; a second expert of the group is named by exactly 24 rows of every block of the group; every other expert is named by at most 24 rows of a block.
All inputs are finite; a program needn't handle non-finite values.
Results may differ from the reference program's by a relative error of at most 0.0065.
Values may be sent and summed in bfloat16 or wider, within the bound.
No kernel may reach another device: no remote copies, remote signals or barrier semaphores. Data moves between devices by JAX's collectives and lax.ppermute only.
A program may use at most 64 MiB of HBM per device.

```python
import math
import jax
import jax.numpy as jnp
from jax import lax

D = 1024
F = 384
TOP = 2
TOK_DEV = 128
EXPERTS = 16
GROUPS = 32
TOKENS = 65536
CAP = 64
COLD = 24


def route_block(block_key, hot_id, second_id):
    order_key, token_key, swap_key = jax.random.split(block_key, 3)
    slot_total = (EXPERTS - 1) * COLD
    needed = TOP * TOK_DEV - CAP
    cold_list = jnp.arange(EXPERTS - 1, dtype=jnp.int32)
    cold_list = jnp.where(cold_list < hot_id, cold_list, cold_list + 1)
    second_place = second_id - (second_id > hot_id).astype(jnp.int32)
    slot_ids = jnp.arange(slot_total, dtype=jnp.int32)
    priority = jax.random.permutation(order_key, slot_total).astype(jnp.int32)
    priority = jnp.where(slot_ids // COLD == second_place, -1 - slot_ids, priority)
    chosen = jnp.sort(jnp.argsort(priority)[:needed])
    cold_picks = cold_list[chosen // COLD]
    sequence = jnp.concatenate([jnp.full((CAP,), hot_id, jnp.int32), cold_picks.astype(jnp.int32)])
    first_pick = sequence[:TOK_DEV]
    second_pick = sequence[TOK_DEV:]
    swap_bits = jax.random.randint(swap_key, (TOK_DEV,), 0, 2)
    left_pick = jnp.where(swap_bits == 1, second_pick, first_pick)
    right_pick = jnp.where(swap_bits == 1, first_pick, second_pick)
    pick_pairs = jnp.stack([left_pick, right_pick], axis=1)
    return pick_pairs[jax.random.permutation(token_key, TOK_DEV)]


def draw_routing(key, part):
    group_count = TOKENS // (TOK_DEV * EXPERTS)
    block_count = group_count * EXPERTS
    hot_key, second_key, block_key = jax.random.split(jax.random.fold_in(key, 17), 3)
    hot_ids = jax.random.randint(hot_key, (group_count,), 0, EXPERTS).astype(jnp.int32)
    second_ids = ((hot_ids + jax.random.randint(second_key, (group_count,), 1, EXPERTS)) % EXPERTS).astype(jnp.int32)
    block_keys = jax.random.split(block_key, block_count)
    block_rows = jax.vmap(route_block)(block_keys, jnp.repeat(hot_ids, EXPERTS), jnp.repeat(second_ids, EXPERTS))
    return block_rows.reshape(TOKENS, TOP).astype(jnp.int32)


def strengthened(array, stream_key, source, target, parts, factor):
    owner, partner = [(jnp.arange(array.shape[dim]) // (array.shape[dim] // parts)).reshape([-1 if axis == dim else 1 for axis in range(array.ndim)]) for dim in (source, target)]
    chosen = jax.random.permutation(stream_key, parts)[partner]
    strong = (owner == chosen) | (owner == (partner + parts // 2) % parts)
    return jnp.where(strong, factor * array, array)


def block_scale(key, extent, cuts, least, largest):
    factor_of = 1.0
    for dim, parts in cuts:
        steps = jax.random.uniform(jax.random.fold_in(jax.random.fold_in(key, 6), dim), (parts,), jnp.float32, least / len(cuts), largest / len(cuts))
        factor_of = factor_of * jnp.repeat(jnp.exp(steps), extent[dim] // parts).reshape((-1,) + (1,) * (len(extent) - 1 - dim))
    return factor_of


def gaussian(own_key, extent, deviation, reach, cuts=(), kind=jnp.bfloat16):
    values = deviation * jax.random.normal(own_key, extent, jnp.float32)
    if cuts:
        values = values * block_scale(own_key, extent, cuts, -0.22, 0.18)
    return jnp.clip(values, -reach, reach).astype(kind)


def noise_with(own_key, shape, width, limit, cuts, heavy, kind=jnp.bfloat16):
    result = width * jax.random.normal(own_key, shape, jnp.float32)
    if cuts:
        result = result * block_scale(own_key, shape, cuts, -0.22, 0.18)
    return jnp.clip(strengthened(result, jax.random.fold_in(own_key, 3), *heavy), -limit, limit).astype(kind)


def setup_inputs(seed: int = 0) -> dict:
    arg_keys = jax.random.split(jax.random.key(seed), 8)
    tokens = noise_with(arg_keys[0], (TOKENS, D), 1.0, 24.0, ((0, 512),), (0, 1, 512, 6.0))
    routing = draw_routing(jax.random.fold_in(arg_keys[7], 71), 0)
    combine = jnp.clip(jnp.exp(math.log(1.0) - 2.3025851 * jax.random.uniform(arg_keys[2], (TOKENS, TOP), jnp.float32) ** block_scale(arg_keys[2], (TOKENS, TOP), ((0, 512),), -0.2, 0.2)), 0.1, 1.0)
    upstream = gaussian(arg_keys[3], (TOKENS, D), 1.0, 6.0, ((0, 512),))
    gate_weight = gaussian(arg_keys[4], (EXPERTS, D, F), D ** -0.5, 0.1875, ((0, 16), (1, 32)))
    up_weight = gaussian(arg_keys[5], (EXPERTS, D, F), D ** -0.5, 0.1875, ((0, 16), (1, 32)))
    down_weight = gaussian(arg_keys[6], (EXPERTS, D, F), F ** -0.5, 0.3125, ((0, 16), (1, 32)))
    return {"tokens": tokens, "routing": routing, "combine": combine, "upstream": upstream, "gate_weight": gate_weight, "up_weight": up_weight, "down_weight": down_weight}


def narrow(values):
    return lax.optimization_barrier(values.astype(jnp.bfloat16))


def reference(tokens, routing, combine, upstream, gate_weight, up_weight, down_weight):
    block_count = TOKENS // TOK_DEV
    pick_total = TOK_DEV * TOP
    gate_wide = gate_weight.astype(jnp.float32)
    up_wide = up_weight.astype(jnp.float32)
    down_wide = down_weight.astype(jnp.float32)
    expert_ids = jnp.arange(EXPERTS, dtype=jnp.int32)

    def block_step(totals, inputs):
        block_tokens, block_routes, block_combine, block_upstream = inputs
        flat_ids = block_routes.reshape(-1).astype(jnp.int32)
        match_table = (flat_ids[:, None] == expert_ids[None, :]).astype(jnp.int32)
        position = jnp.sum((jnp.cumsum(match_table, axis=0) - 1) * match_table, axis=1)
        slot_index = (flat_ids * CAP + position).astype(jnp.int32)
        pick_index = jnp.arange(pick_total, dtype=jnp.int32)
        owners = pick_index // TOP
        token_source = jnp.full((EXPERTS * CAP,), TOK_DEV, jnp.int32).at[slot_index].set(owners)
        pick_source = jnp.full((EXPERTS * CAP,), pick_total, jnp.int32).at[slot_index].set(pick_index)
        input_rows = jnp.take(block_tokens, token_source, axis=0, mode="fill", fill_value=0)
        input_rows = input_rows.reshape(EXPERTS, CAP, D).astype(jnp.float32)
        gate_pre = jnp.einsum("ecd,edf->ecf", input_rows, gate_wide)
        up_pre = jnp.einsum("ecd,edf->ecf", input_rows, up_wide)
        hidden = narrow(jax.nn.silu(gate_pre) * up_pre).astype(jnp.float32)
        results = narrow(jnp.einsum("ecf,edf->ecd", hidden, down_wide)).astype(jnp.float32)
        pick_rows = results.reshape(EXPERTS * CAP, D)[slot_index].reshape(TOK_DEV, TOP, D)
        upstream_wide = block_upstream.astype(jnp.float32)
        layer_rows = jnp.sum(block_combine[:, :, None] * pick_rows, axis=1).astype(jnp.bfloat16)
        combine_rows = jnp.sum(upstream_wide[:, None, :] * pick_rows, axis=2)
        pick_cotangent = narrow(block_combine[:, :, None] * upstream_wide[:, None, :]).reshape(pick_total, D)
        cot_rows = jnp.take(pick_cotangent, pick_source, axis=0, mode="fill", fill_value=0)
        cot_rows = cot_rows.reshape(EXPERTS, CAP, D).astype(jnp.float32)
        hidden_grad = jnp.einsum("ecd,edf->ecf", cot_rows, down_wide)
        sigmoid_value = jax.nn.sigmoid(gate_pre)
        gate_delta = narrow(hidden_grad * up_pre * sigmoid_value * (1.0 + gate_pre * (1.0 - sigmoid_value))).astype(jnp.float32)
        up_delta = narrow(hidden_grad * jax.nn.silu(gate_pre)).astype(jnp.float32)
        input_grads = jnp.einsum("ecf,edf->ecd", gate_delta, gate_wide) + jnp.einsum("ecf,edf->ecd", up_delta, up_wide)
        input_grads = narrow(input_grads).astype(jnp.float32)
        pick_grads = input_grads.reshape(EXPERTS * CAP, D)[slot_index].reshape(TOK_DEV, TOP, D)
        token_rows = jnp.sum(pick_grads, axis=1).astype(jnp.bfloat16)
        gate_total = totals[0] + jnp.einsum("ecd,ecf->edf", input_rows, gate_delta)
        up_total = totals[1] + jnp.einsum("ecd,ecf->edf", input_rows, up_delta)
        return (gate_total, up_total), (layer_rows, token_rows, combine_rows)

    start_totals = (jnp.zeros((EXPERTS, D, F), jnp.float32), jnp.zeros((EXPERTS, D, F), jnp.float32))
    scanned = (tokens.reshape(block_count, TOK_DEV, D), routing.reshape(block_count, TOK_DEV, TOP),
               combine.reshape(block_count, TOK_DEV, TOP), upstream.reshape(block_count, TOK_DEV, D))
    totals, outputs = lax.scan(block_step, start_totals, scanned)
    layer_output = outputs[0].reshape(TOKENS, D)
    token_grad = outputs[1].reshape(TOKENS, D)
    combine_grad = outputs[2].reshape(TOKENS, TOP)
    gate_grad = totals[0] / GROUPS
    up_grad = totals[1] / GROUPS
    return (layer_output, token_grad, combine_grad, gate_grad, up_grad)
```

```python
import jax
import jax.numpy as jnp
from jax import lax
from jax.sharding import PartitionSpec as P


def expert_forward(input_rows, gate_full, up_full, down_full):
    gate_pre = jnp.dot(input_rows, gate_full, preferred_element_type=jnp.float32)
    up_pre = jnp.dot(input_rows, up_full, preferred_element_type=jnp.float32)
    hidden = (jax.nn.silu(gate_pre) * up_pre).astype(jnp.bfloat16)
    results = lax.dot_general(
        hidden, down_full, (((1,), (1,)), ((), ())), preferred_element_type=jnp.float32
    )
    return (results.astype(jnp.bfloat16), gate_pre, up_pre)


def expert_backward(cotangent, gate_pre, up_pre, stacked, down_full):
    hidden_grad = jnp.dot(cotangent, down_full, preferred_element_type=jnp.float32)
    sigmoid_value = jax.nn.sigmoid(gate_pre)
    gate_delta = (
        hidden_grad * up_pre * sigmoid_value * (1.0 + gate_pre * (1.0 - sigmoid_value))
    ).astype(jnp.bfloat16)
    up_delta = (hidden_grad * jax.nn.silu(gate_pre)).astype(jnp.bfloat16)
    deltas = jnp.concatenate([gate_delta, up_delta], axis=1)
    input_grads = lax.dot_general(
        deltas, stacked, (((1,), (1,)), ((), ())), preferred_element_type=jnp.float32
    )
    return (input_grads.astype(jnp.bfloat16), deltas)


def trade_rows(buffer):
    return lax.all_to_all(buffer, "expert", split_axis=0, concat_axis=0, tiled=True)


def pick_slots(routing, expert_total):
    flat_ids = routing.reshape(-1)
    match_table = (flat_ids[:, None] == jnp.arange(expert_total, dtype=jnp.int32)[None, :]).astype(
        jnp.int32
    )
    position = jnp.sum((jnp.cumsum(match_table, axis=0) - 1) * match_table, axis=1)
    expert_loads = jnp.sum(match_table, axis=0)
    return (flat_ids, position, expert_loads)


def shards(tokens, routing, combine, upstream, gate_weight, up_weight, down_weight):
    tok_count = tokens.shape[0]
    top_count = routing.shape[1]
    pick_total = tok_count * top_count
    feature_total = tokens.shape[1]
    hidden_total = gate_weight.shape[2]
    expert_total = lax.axis_size("expert")
    group_total = lax.axis_size("dp")
    capacity = max(tok_count // 2, top_count * tok_count // expert_total + tok_count // 4)
    local_weights = jnp.concatenate([gate_weight[0], up_weight[0], down_weight[0]], axis=1)
    full_weights = lax.all_gather(local_weights, "dp", axis=0, tiled=True)
    gate_full = full_weights[:, :hidden_total]
    up_full = full_weights[:, hidden_total : 2 * hidden_total]
    down_full = full_weights[:, 2 * hidden_total :]
    stacked = full_weights[:, : 2 * hidden_total]
    flat_ids, position, expert_loads = pick_slots(routing, expert_total)
    pick_index = jnp.arange(pick_total, dtype=jnp.int32)
    owners = pick_index // top_count
    upstream_wide = upstream.astype(jnp.float32)
    pick_cotangent = (
        (combine[:, :, None] * upstream_wide[:, None, :])
        .reshape(pick_total, feature_total)
        .astype(jnp.bfloat16)
    )
    slot_index = jnp.where(flat_ids >= 0, flat_ids * capacity + position, expert_total * capacity)
    token_source = (
        jnp.full((expert_total * capacity,), tok_count, jnp.int32)
        .at[slot_index]
        .set(owners, mode="drop")
    )
    pick_source = (
        jnp.full((expert_total * capacity,), pick_total, jnp.int32)
        .at[slot_index]
        .set(pick_index, mode="drop")
    )
    sending = jnp.concatenate(
        [
            jnp.take(tokens, token_source, axis=0, mode="fill", fill_value=0),
            jnp.take(pick_cotangent, pick_source, axis=0, mode="fill", fill_value=0),
        ],
        axis=1,
    )
    arrived_both = trade_rows(
        sending.reshape(expert_total, capacity, 2 * feature_total)
    ).reshape(expert_total * capacity, 2 * feature_total)
    arrived = arrived_both[:, :feature_total]
    cot_arrived = arrived_both[:, feature_total:]
    results, gate_pre, up_pre = expert_forward(arrived, gate_full, up_full, down_full)
    input_grads, deltas = expert_backward(cot_arrived, gate_pre, up_pre, stacked, down_full)
    piece = lax.dot_general(
        arrived, deltas, (((0,), (0,)), ((), ())), preferred_element_type=jnp.float32
    )
    summed = lax.psum_scatter(piece, "dp", scatter_dimension=0, tiled=True) / group_total
    back = jnp.concatenate([results, input_grads], axis=1)
    returned = trade_rows(back.reshape(expert_total, capacity, 2 * feature_total)).reshape(
        expert_total * capacity, 2 * feature_total
    )
    pick_both = jnp.take(returned, slot_index, axis=0, mode="fill", fill_value=0)
    pick_rows = pick_both[:, :feature_total]
    pick_grads = pick_both[:, feature_total:]
    gate_grad = summed[:, :hidden_total][None]
    up_grad = summed[:, hidden_total:][None]
    pick_wide = pick_rows.reshape(tok_count, top_count, feature_total).astype(jnp.float32)
    layer_output = jnp.sum(combine[:, :, None] * pick_wide, axis=1).astype(jnp.bfloat16)
    combine_grad = jnp.sum(upstream_wide[:, None, :] * pick_wide, axis=2)
    token_grad = jnp.sum(
        pick_grads.reshape(tok_count, top_count, feature_total).astype(jnp.float32), axis=1
    ).astype(jnp.bfloat16)
    return (layer_output, token_grad, combine_grad, gate_grad, up_grad)


def solution(mesh):
    placed = (
        P(("dp", "expert"), None),
        P(("dp", "expert"), None),
        P(("dp", "expert"), None),
        P(("dp", "expert"), None),
        P("expert", "dp", None),
        P("expert", "dp", None),
        P("expert", "dp", None),
    )
    return jax.shard_map(
        shards,
        mesh=mesh,
        in_specs=placed,
        out_specs=(
            P(("dp", "expert"), None),
            P(("dp", "expert"), None),
            P(("dp", "expert"), None),
            P("expert", "dp", None),
            P("expert", "dp", None),
        ),
        check_vma=False,
    )
```

```python
import jax
import jax.numpy as jnp
from jax import lax
from jax.sharding import Mesh
from jax.sharding import PartitionSpec as P

DP_AXES = ("y", "xl", "c")
CHIP_AXES = ("y", "xl")
EXPERT_AXES = ("xh", "z")
TOKEN_AXES = DP_AXES + EXPERT_AXES


def expert_forward(input_rows, gate_full, up_full, down_full):
    gate_pre = jnp.dot(input_rows, gate_full, preferred_element_type=jnp.float32)
    up_pre = jnp.dot(input_rows, up_full, preferred_element_type=jnp.float32)
    hidden = (jax.nn.silu(gate_pre) * up_pre).astype(jnp.bfloat16)
    results = lax.dot_general(
        hidden, down_full, (((1,), (1,)), ((), ())), preferred_element_type=jnp.float32
    )
    return (results.astype(jnp.bfloat16), gate_pre, up_pre)


def expert_backward(cotangent, gate_pre, up_pre, stacked, down_full):
    hidden_grad = jnp.dot(cotangent, down_full, preferred_element_type=jnp.float32)
    sigmoid_value = jax.nn.sigmoid(gate_pre)
    gate_delta = (
        hidden_grad * up_pre * sigmoid_value * (1.0 + gate_pre * (1.0 - sigmoid_value))
    ).astype(jnp.bfloat16)
    up_delta = (hidden_grad * jax.nn.silu(gate_pre)).astype(jnp.bfloat16)
    deltas = jnp.concatenate([gate_delta, up_delta], axis=1)
    input_grads = lax.dot_general(
        deltas, stacked, (((1,), (1,)), ((), ())), preferred_element_type=jnp.float32
    )
    return (input_grads.astype(jnp.bfloat16), deltas)


def trade_rows(buffer):
    return lax.all_to_all(buffer, EXPERT_AXES, split_axis=0, concat_axis=0, tiled=True)


def pick_slots(routing, expert_total):
    flat_ids = routing.reshape(-1)
    match_table = (flat_ids[:, None] == jnp.arange(expert_total, dtype=jnp.int32)[None, :]).astype(
        jnp.int32
    )
    position = jnp.sum((jnp.cumsum(match_table, axis=0) - 1) * match_table, axis=1)
    expert_loads = jnp.sum(match_table, axis=0)
    return (flat_ids, position, expert_loads)


def shards(tokens, routing, combine, upstream, gate_weight, up_weight, down_weight):
    tok_count = tokens.shape[0]
    top_count = routing.shape[1]
    pick_total = tok_count * top_count
    feature_total = tokens.shape[1]
    hidden_total = gate_weight.shape[2]
    expert_total = lax.axis_size(EXPERT_AXES)
    group_total = lax.axis_size(DP_AXES)
    core_total = lax.axis_size("c")
    capacity = max(tok_count // 2, top_count * tok_count // expert_total + tok_count // 4)
    local_weights = jnp.concatenate([gate_weight[0], up_weight[0], down_weight[0]], axis=1)
    chip_weights = lax.all_gather(local_weights, CHIP_AXES, axis=0, tiled=False)
    both_weights = lax.all_gather(chip_weights, "c", axis=0, tiled=False)
    full_weights = jnp.swapaxes(both_weights, 0, 1).reshape(-1, local_weights.shape[1])
    gate_full = full_weights[:, :hidden_total]
    up_full = full_weights[:, hidden_total : 2 * hidden_total]
    down_full = full_weights[:, 2 * hidden_total :]
    stacked = full_weights[:, : 2 * hidden_total]
    flat_ids, position, expert_loads = pick_slots(routing, expert_total)
    pick_index = jnp.arange(pick_total, dtype=jnp.int32)
    owners = pick_index // top_count
    upstream_wide = upstream.astype(jnp.float32)
    pick_cotangent = (
        (combine[:, :, None] * upstream_wide[:, None, :])
        .reshape(pick_total, feature_total)
        .astype(jnp.bfloat16)
    )
    slot_index = jnp.where(flat_ids >= 0, flat_ids * capacity + position, expert_total * capacity)
    token_source = (
        jnp.full((expert_total * capacity,), tok_count, jnp.int32)
        .at[slot_index]
        .set(owners, mode="drop")
    )
    pick_source = (
        jnp.full((expert_total * capacity,), pick_total, jnp.int32)
        .at[slot_index]
        .set(pick_index, mode="drop")
    )
    sending = jnp.concatenate(
        [
            jnp.take(tokens, token_source, axis=0, mode="fill", fill_value=0),
            jnp.take(pick_cotangent, pick_source, axis=0, mode="fill", fill_value=0),
        ],
        axis=1,
    )
    arrived_both = trade_rows(
        sending.reshape(expert_total, capacity, 2 * feature_total)
    ).reshape(expert_total * capacity, 2 * feature_total)
    arrived = arrived_both[:, :feature_total]
    cot_arrived = arrived_both[:, feature_total:]
    results, gate_pre, up_pre = expert_forward(arrived, gate_full, up_full, down_full)
    input_grads, deltas = expert_backward(cot_arrived, gate_pre, up_pre, stacked, down_full)
    piece = lax.dot_general(
        arrived, deltas, (((0,), (0,)), ((), ())), preferred_element_type=jnp.float32
    )
    slice_rows = gate_weight.shape[1]
    by_core = jnp.swapaxes(
        piece.reshape(group_total // core_total, core_total, slice_rows, 2 * hidden_total), 0, 1
    )
    core_summed = lax.psum_scatter(by_core, "c", scatter_dimension=0, tiled=True)
    summed = lax.psum_scatter(
        core_summed.reshape(group_total // core_total, slice_rows, 2 * hidden_total),
        CHIP_AXES,
        scatter_dimension=0,
        tiled=True,
    )
    summed = summed.reshape(slice_rows, 2 * hidden_total) / group_total
    back = jnp.concatenate([results, input_grads], axis=1)
    returned = trade_rows(back.reshape(expert_total, capacity, 2 * feature_total)).reshape(
        expert_total * capacity, 2 * feature_total
    )
    pick_both = jnp.take(returned, slot_index, axis=0, mode="fill", fill_value=0)
    pick_rows = pick_both[:, :feature_total]
    pick_grads = pick_both[:, feature_total:]
    gate_grad = summed[:, :hidden_total][None]
    up_grad = summed[:, hidden_total:][None]
    pick_wide = pick_rows.reshape(tok_count, top_count, feature_total).astype(jnp.float32)
    layer_output = jnp.sum(combine[:, :, None] * pick_wide, axis=1).astype(jnp.bfloat16)
    combine_grad = jnp.sum(upstream_wide[:, None, :] * pick_wide, axis=2)
    token_grad = jnp.sum(
        pick_grads.reshape(tok_count, top_count, feature_total).astype(jnp.float32), axis=1
    ).astype(jnp.bfloat16)
    return (layer_output, token_grad, combine_grad, gate_grad, up_grad)


def solution(mesh):
    dp_size = mesh.shape["dp"]
    expert_size = mesh.shape["expert"]
    fine = Mesh(
        mesh.devices.reshape(dp_size // 4, 2, 2, 2, expert_size // 2),
        DP_AXES + EXPERT_AXES,
    )
    placed = (
        P(TOKEN_AXES, None),
        P(TOKEN_AXES, None),
        P(TOKEN_AXES, None),
        P(TOKEN_AXES, None),
        P(EXPERT_AXES, DP_AXES, None),
        P(EXPERT_AXES, DP_AXES, None),
        P(EXPERT_AXES, DP_AXES, None),
    )
    return jax.shard_map(
        shards,
        mesh=fine,
        in_specs=placed,
        out_specs=(
            P(TOKEN_AXES, None),
            P(TOKEN_AXES, None),
            P(TOKEN_AXES, None),
            P(EXPERT_AXES, DP_AXES, None),
            P(EXPERT_AXES, DP_AXES, None),
        ),
        check_vma=False,
    )
```

```python
import jax
import jax.numpy as jnp
from jax import lax
from jax.sharding import Mesh
from jax.sharding import PartitionSpec as P

DP_AXES = ("y", "xl", "c")
CHIP_AXES = ("y", "xl")
EXPERT_AXES = ("xh", "z")
TOKEN_AXES = DP_AXES + EXPERT_AXES


def expert_forward(input_rows, gate_full, up_full, down_full):
    gate_pre = jnp.dot(input_rows, gate_full, preferred_element_type=jnp.float32)
    up_pre = jnp.dot(input_rows, up_full, preferred_element_type=jnp.float32)
    hidden = (jax.nn.silu(gate_pre) * up_pre).astype(jnp.bfloat16)
    results = lax.dot_general(
        hidden, down_full, (((1,), (1,)), ((), ())), preferred_element_type=jnp.float32
    )
    return (results.astype(jnp.bfloat16), gate_pre, up_pre)


def expert_backward(cotangent, gate_pre, up_pre, stacked, down_full):
    hidden_grad = jnp.dot(cotangent, down_full, preferred_element_type=jnp.float32)
    sigmoid_value = jax.nn.sigmoid(gate_pre)
    gate_delta = (
        hidden_grad * up_pre * sigmoid_value * (1.0 + gate_pre * (1.0 - sigmoid_value))
    ).astype(jnp.bfloat16)
    up_delta = (hidden_grad * jax.nn.silu(gate_pre)).astype(jnp.bfloat16)
    deltas = jnp.concatenate([gate_delta, up_delta], axis=1)
    input_grads = lax.dot_general(
        deltas, stacked, (((1,), (1,)), ((), ())), preferred_element_type=jnp.float32
    )
    return (input_grads.astype(jnp.bfloat16), deltas)


def trade_rows(buffer):
    return lax.all_to_all(buffer, EXPERT_AXES, split_axis=0, concat_axis=0, tiled=True)


def pick_slots(routing, expert_total):
    flat_ids = routing.reshape(-1)
    match_table = (flat_ids[:, None] == jnp.arange(expert_total, dtype=jnp.int32)[None, :]).astype(
        jnp.int32
    )
    position = jnp.sum((jnp.cumsum(match_table, axis=0) - 1) * match_table, axis=1)
    expert_loads = jnp.sum(match_table, axis=0)
    return (flat_ids, position, expert_loads)


def shards(tokens, routing, combine, upstream, gate_weight, up_weight, down_weight):
    tok_count = tokens.shape[0]
    top_count = routing.shape[1]
    pick_total = tok_count * top_count
    feature_total = tokens.shape[1]
    hidden_total = gate_weight.shape[2]
    expert_total = lax.axis_size(EXPERT_AXES)
    group_total = lax.axis_size(DP_AXES)
    core_total = lax.axis_size("c")
    capacity = max(tok_count // 2, top_count * tok_count // expert_total + tok_count // 4)
    local_weights = jnp.concatenate([gate_weight[0], up_weight[0], down_weight[0]], axis=1)
    full_weights = lax.all_gather(local_weights, DP_AXES, axis=0, tiled=True)
    gate_full = full_weights[:, :hidden_total]
    up_full = full_weights[:, hidden_total : 2 * hidden_total]
    down_full = full_weights[:, 2 * hidden_total :]
    stacked = full_weights[:, : 2 * hidden_total]
    flat_ids, position, expert_loads = pick_slots(routing, expert_total)
    pick_index = jnp.arange(pick_total, dtype=jnp.int32)
    owners = pick_index // top_count
    upstream_wide = upstream.astype(jnp.float32)
    pick_cotangent = (
        (combine[:, :, None] * upstream_wide[:, None, :])
        .reshape(pick_total, feature_total)
        .astype(jnp.bfloat16)
    )
    slot_index = jnp.where(flat_ids >= 0, flat_ids * capacity + position, expert_total * capacity)
    token_source = (
        jnp.full((expert_total * capacity,), tok_count, jnp.int32)
        .at[slot_index]
        .set(owners, mode="drop")
    )
    pick_source = (
        jnp.full((expert_total * capacity,), pick_total, jnp.int32)
        .at[slot_index]
        .set(pick_index, mode="drop")
    )
    sending = jnp.concatenate(
        [
            jnp.take(tokens, token_source, axis=0, mode="fill", fill_value=0),
            jnp.take(pick_cotangent, pick_source, axis=0, mode="fill", fill_value=0),
        ],
        axis=1,
    )
    arrived_both = trade_rows(
        sending.reshape(expert_total, capacity, 2 * feature_total)
    ).reshape(expert_total * capacity, 2 * feature_total)
    arrived = arrived_both[:, :feature_total]
    cot_arrived = arrived_both[:, feature_total:]
    results, gate_pre, up_pre = expert_forward(arrived, gate_full, up_full, down_full)
    input_grads, deltas = expert_backward(cot_arrived, gate_pre, up_pre, stacked, down_full)
    piece = lax.dot_general(
        arrived, deltas, (((0,), (0,)), ((), ())), preferred_element_type=jnp.float32
    )
    slice_rows = gate_weight.shape[1]
    by_core = jnp.swapaxes(
        piece.reshape(group_total // core_total, core_total, slice_rows, 2 * hidden_total), 0, 1
    )
    core_summed = lax.psum_scatter(by_core, "c", scatter_dimension=0, tiled=True)
    summed = lax.psum_scatter(
        core_summed.reshape(group_total // core_total, slice_rows, 2 * hidden_total),
        CHIP_AXES,
        scatter_dimension=0,
        tiled=True,
    )
    summed = summed.reshape(slice_rows, 2 * hidden_total) / group_total
    back = jnp.concatenate([results, input_grads], axis=1)
    returned = trade_rows(back.reshape(expert_total, capacity, 2 * feature_total)).reshape(
        expert_total * capacity, 2 * feature_total
    )
    pick_both = jnp.take(returned, slot_index, axis=0, mode="fill", fill_value=0)
    pick_rows = pick_both[:, :feature_total]
    pick_grads = pick_both[:, feature_total:]
    gate_grad = summed[:, :hidden_total][None]
    up_grad = summed[:, hidden_total:][None]
    pick_wide = pick_rows.reshape(tok_count, top_count, feature_total).astype(jnp.float32)
    layer_output = jnp.sum(combine[:, :, None] * pick_wide, axis=1).astype(jnp.bfloat16)
    combine_grad = jnp.sum(upstream_wide[:, None, :] * pick_wide, axis=2)
    token_grad = jnp.sum(
        pick_grads.reshape(tok_count, top_count, feature_total).astype(jnp.float32), axis=1
    ).astype(jnp.bfloat16)
    return (layer_output, token_grad, combine_grad, gate_grad, up_grad)


def solution(mesh):
    dp_size = mesh.shape["dp"]
    expert_size = mesh.shape["expert"]
    fine = Mesh(
        mesh.devices.reshape(dp_size // 4, 2, 2, 2, expert_size // 2),
        DP_AXES + EXPERT_AXES,
    )
    placed = (
        P(TOKEN_AXES, None),
        P(TOKEN_AXES, None),
        P(TOKEN_AXES, None),
        P(TOKEN_AXES, None),
        P(EXPERT_AXES, DP_AXES, None),
        P(EXPERT_AXES, DP_AXES, None),
        P(EXPERT_AXES, DP_AXES, None),
    )
    return jax.shard_map(
        shards,
        mesh=fine,
        in_specs=placed,
        out_specs=(
            P(TOKEN_AXES, None),
            P(TOKEN_AXES, None),
            P(TOKEN_AXES, None),
            P(EXPERT_AXES, DP_AXES, None),
            P(EXPERT_AXES, DP_AXES, None),
        ),
        check_vma=False,
    )
```

```python
import jax
import jax.numpy as jnp
from jax import lax
from jax.sharding import Mesh
from jax.sharding import PartitionSpec as P

DP_AXES = ("y", "xl", "c")
CHIP_AXES = ("y", "xl")
EXPERT_AXES = ("xh", "z")
TOKEN_AXES = DP_AXES + EXPERT_AXES


def expert_forward(input_rows, gate_full, up_full, down_full):
    gate_pre = jnp.dot(input_rows, gate_full, preferred_element_type=jnp.float32)
    up_pre = jnp.dot(input_rows, up_full, preferred_element_type=jnp.float32)
    hidden = (jax.nn.silu(gate_pre) * up_pre).astype(jnp.bfloat16)
    results = lax.dot_general(
        hidden, down_full, (((1,), (1,)), ((), ())), preferred_element_type=jnp.float32
    )
    return (results.astype(jnp.bfloat16), gate_pre, up_pre)


def expert_backward(cotangent, gate_pre, up_pre, stacked, down_full):
    hidden_grad = jnp.dot(cotangent, down_full, preferred_element_type=jnp.float32)
    sigmoid_value = jax.nn.sigmoid(gate_pre)
    gate_delta = (
        hidden_grad * up_pre * sigmoid_value * (1.0 + gate_pre * (1.0 - sigmoid_value))
    ).astype(jnp.bfloat16)
    up_delta = (hidden_grad * jax.nn.silu(gate_pre)).astype(jnp.bfloat16)
    deltas = jnp.concatenate([gate_delta, up_delta], axis=1)
    input_grads = lax.dot_general(
        deltas, stacked, (((1,), (1,)), ((), ())), preferred_element_type=jnp.float32
    )
    return (input_grads.astype(jnp.bfloat16), deltas)


def trade_rows(buffer):
    return lax.all_to_all(buffer, EXPERT_AXES, split_axis=0, concat_axis=0, tiled=True)


def pick_slots(routing, expert_total):
    flat_ids = routing.reshape(-1)
    match_table = (flat_ids[:, None] == jnp.arange(expert_total, dtype=jnp.int32)[None, :]).astype(
        jnp.int32
    )
    position = jnp.sum((jnp.cumsum(match_table, axis=0) - 1) * match_table, axis=1)
    expert_loads = jnp.sum(match_table, axis=0)
    return (flat_ids, position, expert_loads)


def shards(tokens, routing, combine, upstream, gate_weight, up_weight, down_weight):
    tok_count = tokens.shape[0]
    top_count = routing.shape[1]
    pick_total = tok_count * top_count
    feature_total = tokens.shape[1]
    hidden_total = gate_weight.shape[2]
    expert_total = lax.axis_size(EXPERT_AXES)
    group_total = lax.axis_size(DP_AXES)
    core_total = lax.axis_size("c")
    capacity = max(tok_count // 2, top_count * tok_count // expert_total + tok_count // 4)
    local_weights = jnp.concatenate([gate_weight[0], up_weight[0], down_weight[0]], axis=1)
    full_weights = lax.all_gather(local_weights, DP_AXES, axis=0, tiled=True)
    gate_full = full_weights[:, :hidden_total]
    up_full = full_weights[:, hidden_total : 2 * hidden_total]
    down_full = full_weights[:, 2 * hidden_total :]
    stacked = full_weights[:, : 2 * hidden_total]
    flat_ids, position, expert_loads = pick_slots(routing, expert_total)
    pick_index = jnp.arange(pick_total, dtype=jnp.int32)
    owners = pick_index // top_count
    upstream_wide = upstream.astype(jnp.float32)
    pick_cotangent = (
        (combine[:, :, None] * upstream_wide[:, None, :])
        .reshape(pick_total, feature_total)
        .astype(jnp.bfloat16)
    )
    slot_index = jnp.where(flat_ids >= 0, flat_ids * capacity + position, expert_total * capacity)
    token_source = (
        jnp.full((expert_total * capacity,), tok_count, jnp.int32)
        .at[slot_index]
        .set(owners, mode="drop")
    )
    pick_source = (
        jnp.full((expert_total * capacity,), pick_total, jnp.int32)
        .at[slot_index]
        .set(pick_index, mode="drop")
    )
    chunk_total = 2
    chunk_rows = capacity // chunk_total
    token_slots = token_source.reshape(expert_total, capacity)
    pick_slots_of = pick_source.reshape(expert_total, capacity)
    returned_parts = []
    pieces = []
    for chunk in range(chunk_total):
        window = slice(chunk * chunk_rows, (chunk + 1) * chunk_rows)
        sending = jnp.concatenate(
            [
                jnp.take(tokens, token_slots[:, window], axis=0, mode="fill", fill_value=0),
                jnp.take(pick_cotangent, pick_slots_of[:, window], axis=0, mode="fill", fill_value=0),
            ],
            axis=2,
        )
        arrived_both = trade_rows(sending).reshape(expert_total * chunk_rows, 2 * feature_total)
        arrived = arrived_both[:, :feature_total]
        cot_arrived = arrived_both[:, feature_total:]
        results, gate_pre, up_pre = expert_forward(arrived, gate_full, up_full, down_full)
        input_grads, deltas = expert_backward(cot_arrived, gate_pre, up_pre, stacked, down_full)
        pieces.append(
            lax.dot_general(
                arrived, deltas, (((0,), (0,)), ((), ())), preferred_element_type=jnp.float32
            )
        )
        back = jnp.concatenate([results, input_grads], axis=1)
        returned_parts.append(
            trade_rows(back.reshape(expert_total, chunk_rows, 2 * feature_total))
        )
    piece = pieces[0]
    for extra in pieces[1:]:
        piece = piece + extra
    slice_rows = gate_weight.shape[1]
    by_core = jnp.swapaxes(
        piece.reshape(group_total // core_total, core_total, slice_rows, 2 * hidden_total), 0, 1
    )
    core_summed = lax.psum_scatter(by_core, "c", scatter_dimension=0, tiled=True)
    summed = lax.psum_scatter(
        core_summed.reshape(group_total // core_total, slice_rows, 2 * hidden_total),
        CHIP_AXES,
        scatter_dimension=0,
        tiled=True,
    )
    summed = summed.reshape(slice_rows, 2 * hidden_total) / group_total
    returned = jnp.concatenate(returned_parts, axis=1).reshape(
        expert_total * capacity, 2 * feature_total
    )
    pick_both = jnp.take(returned, slot_index, axis=0, mode="fill", fill_value=0)
    pick_rows = pick_both[:, :feature_total]
    pick_grads = pick_both[:, feature_total:]
    gate_grad = summed[:, :hidden_total][None]
    up_grad = summed[:, hidden_total:][None]
    pick_wide = pick_rows.reshape(tok_count, top_count, feature_total).astype(jnp.float32)
    layer_output = jnp.sum(combine[:, :, None] * pick_wide, axis=1).astype(jnp.bfloat16)
    combine_grad = jnp.sum(upstream_wide[:, None, :] * pick_wide, axis=2)
    token_grad = jnp.sum(
        pick_grads.reshape(tok_count, top_count, feature_total).astype(jnp.float32), axis=1
    ).astype(jnp.bfloat16)
    return (layer_output, token_grad, combine_grad, gate_grad, up_grad)


def solution(mesh):
    dp_size = mesh.shape["dp"]
    expert_size = mesh.shape["expert"]
    fine = Mesh(
        mesh.devices.reshape(dp_size // 4, 2, 2, 2, expert_size // 2),
        DP_AXES + EXPERT_AXES,
    )
    placed = (
        P(TOKEN_AXES, None),
        P(TOKEN_AXES, None),
        P(TOKEN_AXES, None),
        P(TOKEN_AXES, None),
        P(EXPERT_AXES, DP_AXES, None),
        P(EXPERT_AXES, DP_AXES, None),
        P(EXPERT_AXES, DP_AXES, None),
    )
    return jax.shard_map(
        shards,
        mesh=fine,
        in_specs=placed,
        out_specs=(
            P(TOKEN_AXES, None),
            P(TOKEN_AXES, None),
            P(TOKEN_AXES, None),
            P(EXPERT_AXES, DP_AXES, None),
            P(EXPERT_AXES, DP_AXES, None),
        ),
        check_vma=False,
    )
```

```python
import jax
import jax.numpy as jnp
from jax import lax
from jax.sharding import Mesh
from jax.sharding import PartitionSpec as P

DP_AXES = ("y", "xl", "c")
CHIP_AXES = ("y", "xl")
EXPERT_AXES = ("xh", "z")
TOKEN_AXES = DP_AXES + EXPERT_AXES


def expert_forward(input_rows, gate_full, up_full, down_full):
    gate_pre = jnp.dot(input_rows, gate_full, preferred_element_type=jnp.float32)
    up_pre = jnp.dot(input_rows, up_full, preferred_element_type=jnp.float32)
    hidden = (jax.nn.silu(gate_pre) * up_pre).astype(jnp.bfloat16)
    results = lax.dot_general(
        hidden, down_full, (((1,), (1,)), ((), ())), preferred_element_type=jnp.float32
    )
    return (results.astype(jnp.bfloat16), gate_pre, up_pre)


def expert_backward(cotangent, gate_pre, up_pre, stacked, down_full):
    hidden_grad = jnp.dot(cotangent, down_full, preferred_element_type=jnp.float32)
    sigmoid_value = jax.nn.sigmoid(gate_pre)
    gate_delta = (
        hidden_grad * up_pre * sigmoid_value * (1.0 + gate_pre * (1.0 - sigmoid_value))
    ).astype(jnp.bfloat16)
    up_delta = (hidden_grad * jax.nn.silu(gate_pre)).astype(jnp.bfloat16)
    deltas = jnp.concatenate([gate_delta, up_delta], axis=1)
    input_grads = lax.dot_general(
        deltas, stacked, (((1,), (1,)), ((), ())), preferred_element_type=jnp.float32
    )
    return (input_grads.astype(jnp.bfloat16), deltas)


def trade_rows(buffer):
    return lax.all_to_all(buffer, EXPERT_AXES, split_axis=0, concat_axis=0, tiled=True)


def pick_slots(routing, expert_total):
    flat_ids = routing.reshape(-1)
    match_table = (flat_ids[:, None] == jnp.arange(expert_total, dtype=jnp.int32)[None, :]).astype(
        jnp.int32
    )
    position = jnp.sum((jnp.cumsum(match_table, axis=0) - 1) * match_table, axis=1)
    expert_loads = jnp.sum(match_table, axis=0)
    return (flat_ids, position, expert_loads)


def shards(tokens, routing, combine, upstream, gate_weight, up_weight, down_weight):
    tok_count = tokens.shape[0]
    top_count = routing.shape[1]
    pick_total = tok_count * top_count
    feature_total = tokens.shape[1]
    hidden_total = gate_weight.shape[2]
    expert_total = lax.axis_size(EXPERT_AXES)
    group_total = lax.axis_size(DP_AXES)
    core_total = lax.axis_size("c")
    capacity = max(tok_count // 2, top_count * tok_count // expert_total + tok_count // 4)
    local_weights = jnp.concatenate([gate_weight[0], up_weight[0], down_weight[0]], axis=1)
    full_weights = lax.all_gather(local_weights, DP_AXES, axis=0, tiled=True)
    gate_full = full_weights[:, :hidden_total]
    up_full = full_weights[:, hidden_total : 2 * hidden_total]
    down_full = full_weights[:, 2 * hidden_total :]
    stacked = full_weights[:, : 2 * hidden_total]
    flat_ids, position, expert_loads = pick_slots(routing, expert_total)
    upstream_wide = upstream.astype(jnp.float32)
    pick_cotangent = (
        (combine[:, :, None] * upstream_wide[:, None, :])
        .reshape(pick_total, feature_total)
        .astype(jnp.bfloat16)
    )
    slot_index = flat_ids * capacity + position
    select = (
        slot_index[None, :] == jnp.arange(expert_total * capacity, dtype=jnp.int32)[:, None]
    ).astype(jnp.bfloat16)
    payload = jnp.concatenate([jnp.repeat(tokens, top_count, axis=0), pick_cotangent], axis=1)
    sending = jnp.dot(select, payload, preferred_element_type=jnp.float32).astype(jnp.bfloat16)
    arrived_both = trade_rows(
        sending.reshape(expert_total, capacity, 2 * feature_total)
    ).reshape(expert_total * capacity, 2 * feature_total)
    arrived = arrived_both[:, :feature_total]
    cot_arrived = arrived_both[:, feature_total:]
    results, gate_pre, up_pre = expert_forward(arrived, gate_full, up_full, down_full)
    input_grads, deltas = expert_backward(cot_arrived, gate_pre, up_pre, stacked, down_full)
    piece = lax.dot_general(
        arrived, deltas, (((0,), (0,)), ((), ())), preferred_element_type=jnp.float32
    )
    slice_rows = gate_weight.shape[1]
    by_core = jnp.swapaxes(
        piece.reshape(group_total // core_total, core_total, slice_rows, 2 * hidden_total), 0, 1
    )
    core_summed = lax.psum_scatter(by_core, "c", scatter_dimension=0, tiled=True)
    summed = lax.psum_scatter(
        core_summed.reshape(group_total // core_total, slice_rows, 2 * hidden_total),
        CHIP_AXES,
        scatter_dimension=0,
        tiled=True,
    )
    summed = summed.reshape(slice_rows, 2 * hidden_total) / group_total
    back = jnp.concatenate([results, input_grads], axis=1)
    returned = trade_rows(back.reshape(expert_total, capacity, 2 * feature_total)).reshape(
        expert_total * capacity, 2 * feature_total
    )
    pick_both = lax.dot_general(
        select, returned, (((0,), (0,)), ((), ())), preferred_element_type=jnp.float32
    )
    pick_rows = pick_both[:, :feature_total]
    pick_grads = pick_both[:, feature_total:]
    gate_grad = summed[:, :hidden_total][None]
    up_grad = summed[:, hidden_total:][None]
    pick_wide = pick_rows.reshape(tok_count, top_count, feature_total)
    layer_output = jnp.sum(combine[:, :, None] * pick_wide, axis=1).astype(jnp.bfloat16)
    combine_grad = jnp.sum(upstream_wide[:, None, :] * pick_wide, axis=2)
    token_grad = jnp.sum(
        pick_grads.reshape(tok_count, top_count, feature_total), axis=1
    ).astype(jnp.bfloat16)
    return (layer_output, token_grad, combine_grad, gate_grad, up_grad)


def solution(mesh):
    dp_size = mesh.shape["dp"]
    expert_size = mesh.shape["expert"]
    fine = Mesh(
        mesh.devices.reshape(dp_size // 4, 2, 2, 2, expert_size // 2),
        DP_AXES + EXPERT_AXES,
    )
    placed = (
        P(TOKEN_AXES, None),
        P(TOKEN_AXES, None),
        P(TOKEN_AXES, None),
        P(TOKEN_AXES, None),
        P(EXPERT_AXES, DP_AXES, None),
        P(EXPERT_AXES, DP_AXES, None),
        P(EXPERT_AXES, DP_AXES, None),
    )
    return jax.shard_map(
        shards,
        mesh=fine,
        in_specs=placed,
        out_specs=(
            P(TOKEN_AXES, None),
            P(TOKEN_AXES, None),
            P(TOKEN_AXES, None),
            P(EXPERT_AXES, DP_AXES, None),
            P(EXPERT_AXES, DP_AXES, None),
        ),
        check_vma=False,
    )
```

```python
import jax
import jax.numpy as jnp
from jax import lax
from jax.experimental.layout import Layout, with_layout_constraint
from jax.sharding import Mesh
from jax.sharding import PartitionSpec as P

DP_AXES = ("y", "xl", "c")
CHIP_AXES = ("y", "xl")
EXPERT_AXES = ("xh", "z")
TOKEN_AXES = DP_AXES + EXPERT_AXES


def expert_forward(input_rows, gate_full, up_full, down_full):
    gate_pre = jnp.dot(input_rows, gate_full, preferred_element_type=jnp.float32)
    up_pre = jnp.dot(input_rows, up_full, preferred_element_type=jnp.float32)
    hidden = (jax.nn.silu(gate_pre) * up_pre).astype(jnp.bfloat16)
    results = lax.dot_general(
        hidden, down_full, (((1,), (1,)), ((), ())), preferred_element_type=jnp.float32
    )
    return (results.astype(jnp.bfloat16), gate_pre, up_pre)


def expert_backward(cotangent, gate_pre, up_pre, stacked, down_full):
    hidden_grad = jnp.dot(cotangent, down_full, preferred_element_type=jnp.float32)
    sigmoid_value = jax.nn.sigmoid(gate_pre)
    gate_delta = (
        hidden_grad * up_pre * sigmoid_value * (1.0 + gate_pre * (1.0 - sigmoid_value))
    ).astype(jnp.bfloat16)
    up_delta = (hidden_grad * jax.nn.silu(gate_pre)).astype(jnp.bfloat16)
    deltas = jnp.concatenate([gate_delta, up_delta], axis=1)
    input_grads = lax.dot_general(
        deltas, stacked, (((1,), (1,)), ((), ())), preferred_element_type=jnp.float32
    )
    return (input_grads.astype(jnp.bfloat16), deltas)


def trade_rows(buffer):
    return lax.all_to_all(buffer, EXPERT_AXES, split_axis=0, concat_axis=0, tiled=True)


def pick_slots(routing, expert_total):
    flat_ids = routing.reshape(-1)
    match_table = (flat_ids[:, None] == jnp.arange(expert_total, dtype=jnp.int32)[None, :]).astype(
        jnp.int32
    )
    position = jnp.sum((jnp.cumsum(match_table, axis=0) - 1) * match_table, axis=1)
    expert_loads = jnp.sum(match_table, axis=0)
    return (flat_ids, position, expert_loads)


def shards(tokens, routing, combine, upstream, gate_weight, up_weight, down_weight):
    tok_count = tokens.shape[0]
    top_count = routing.shape[1]
    pick_total = tok_count * top_count
    feature_total = tokens.shape[1]
    hidden_total = gate_weight.shape[2]
    expert_total = lax.axis_size(EXPERT_AXES)
    group_total = lax.axis_size(DP_AXES)
    core_total = lax.axis_size("c")
    capacity = max(tok_count // 2, top_count * tok_count // expert_total + tok_count // 4)
    local_weights = jnp.concatenate([gate_weight[0], up_weight[0], down_weight[0]], axis=1)
    full_weights = lax.all_gather(local_weights, DP_AXES, axis=0, tiled=True)
    gate_full = full_weights[:, :hidden_total]
    up_full = full_weights[:, hidden_total : 2 * hidden_total]
    down_full = full_weights[:, 2 * hidden_total :]
    stacked = full_weights[:, : 2 * hidden_total]
    flat_ids, position, expert_loads = pick_slots(routing, expert_total)
    upstream_wide = upstream.astype(jnp.float32)
    pick_cotangent = (
        (combine[:, :, None] * upstream_wide[:, None, :])
        .reshape(pick_total, feature_total)
        .astype(jnp.bfloat16)
    )
    slot_index = flat_ids * capacity + position
    select = (
        slot_index[None, :] == jnp.arange(expert_total * capacity, dtype=jnp.int32)[:, None]
    ).astype(jnp.bfloat16)
    payload = jnp.concatenate([jnp.repeat(tokens, top_count, axis=0), pick_cotangent], axis=1)
    sending = jnp.dot(select, payload, preferred_element_type=jnp.float32).astype(jnp.bfloat16)
    arrived_both = trade_rows(
        sending.reshape(expert_total, capacity, 2 * feature_total)
    ).reshape(expert_total * capacity, 2 * feature_total)
    arrived = arrived_both[:, :feature_total]
    cot_arrived = arrived_both[:, feature_total:]
    results, gate_pre, up_pre = expert_forward(arrived, gate_full, up_full, down_full)
    input_grads, deltas = expert_backward(cot_arrived, gate_pre, up_pre, stacked, down_full)
    piece = lax.dot_general(
        arrived, deltas, (((0,), (0,)), ((), ())), preferred_element_type=jnp.float32
    )
    slice_rows = gate_weight.shape[1]
    by_core = jnp.swapaxes(
        piece.reshape(group_total // core_total, core_total, slice_rows, 2 * hidden_total), 0, 1
    )
    core_summed = lax.psum_scatter(by_core, "c", scatter_dimension=0, tiled=True)
    summed = lax.psum_scatter(
        core_summed.reshape(group_total // core_total, slice_rows, 2 * hidden_total),
        CHIP_AXES,
        scatter_dimension=0,
        tiled=True,
    )
    summed = summed.reshape(slice_rows, 2 * hidden_total) / group_total
    row_major = Layout(major_to_minor=(0, 1))
    back = jnp.concatenate(
        [with_layout_constraint(results, row_major), with_layout_constraint(input_grads, row_major)],
        axis=1,
    )
    returned = trade_rows(back.reshape(expert_total, capacity, 2 * feature_total)).reshape(
        expert_total * capacity, 2 * feature_total
    )
    pick_both = lax.dot_general(
        select, returned, (((0,), (0,)), ((), ())), preferred_element_type=jnp.float32
    )
    pick_rows = pick_both[:, :feature_total]
    pick_grads = pick_both[:, feature_total:]
    gate_grad = summed[:, :hidden_total][None]
    up_grad = summed[:, hidden_total:][None]
    pick_wide = pick_rows.reshape(tok_count, top_count, feature_total)
    layer_output = jnp.sum(combine[:, :, None] * pick_wide, axis=1).astype(jnp.bfloat16)
    combine_grad = jnp.sum(upstream_wide[:, None, :] * pick_wide, axis=2)
    token_grad = jnp.sum(
        pick_grads.reshape(tok_count, top_count, feature_total), axis=1
    ).astype(jnp.bfloat16)
    return (layer_output, token_grad, combine_grad, gate_grad, up_grad)


def solution(mesh):
    dp_size = mesh.shape["dp"]
    expert_size = mesh.shape["expert"]
    fine = Mesh(
        mesh.devices.reshape(dp_size // 4, 2, 2, 2, expert_size // 2),
        DP_AXES + EXPERT_AXES,
    )
    placed = (
        P(TOKEN_AXES, None),
        P(TOKEN_AXES, None),
        P(TOKEN_AXES, None),
        P(TOKEN_AXES, None),
        P(EXPERT_AXES, DP_AXES, None),
        P(EXPERT_AXES, DP_AXES, None),
        P(EXPERT_AXES, DP_AXES, None),
    )
    return jax.shard_map(
        shards,
        mesh=fine,
        in_specs=placed,
        out_specs=(
            P(TOKEN_AXES, None),
            P(TOKEN_AXES, None),
            P(TOKEN_AXES, None),
            P(EXPERT_AXES, DP_AXES, None),
            P(EXPERT_AXES, DP_AXES, None),
        ),
        check_vma=False,
    )
```

```python
import jax
import jax.numpy as jnp
from jax import lax
from jax.experimental.layout import Layout, with_layout_constraint
from jax.sharding import Mesh
from jax.sharding import PartitionSpec as P

DP_AXES = ("y", "xl", "c")
CHIP_AXES = ("y", "xl")
EXPERT_AXES = ("xh", "z")
TOKEN_AXES = DP_AXES + EXPERT_AXES


def expert_forward(input_rows, stacked, down_full):
    hidden_total = stacked.shape[1] // 2
    both_pre = jnp.dot(input_rows, stacked, preferred_element_type=jnp.float32)
    gate_pre = both_pre[:, :hidden_total]
    up_pre = both_pre[:, hidden_total:]
    hidden = (jax.nn.silu(gate_pre) * up_pre).astype(jnp.bfloat16)
    results = lax.dot_general(
        hidden, down_full, (((1,), (1,)), ((), ())), preferred_element_type=jnp.float32
    )
    return (results.astype(jnp.bfloat16), gate_pre, up_pre)


def expert_backward(cotangent, gate_pre, up_pre, stacked, down_full):
    hidden_grad = jnp.dot(cotangent, down_full, preferred_element_type=jnp.float32)
    sigmoid_value = jax.nn.sigmoid(gate_pre)
    gate_delta = (
        hidden_grad * up_pre * sigmoid_value * (1.0 + gate_pre * (1.0 - sigmoid_value))
    ).astype(jnp.bfloat16)
    up_delta = (hidden_grad * jax.nn.silu(gate_pre)).astype(jnp.bfloat16)
    deltas = jnp.concatenate([gate_delta, up_delta], axis=1)
    input_grads = lax.dot_general(
        deltas, stacked, (((1,), (1,)), ((), ())), preferred_element_type=jnp.float32
    )
    return (input_grads.astype(jnp.bfloat16), deltas)


def trade_rows(buffer):
    return lax.all_to_all(buffer, EXPERT_AXES, split_axis=0, concat_axis=0, tiled=True)


def pick_slots(routing, expert_total):
    flat_ids = routing.reshape(-1)
    match_table = (flat_ids[:, None] == jnp.arange(expert_total, dtype=jnp.int32)[None, :]).astype(
        jnp.int32
    )
    position = jnp.sum((jnp.cumsum(match_table, axis=0) - 1) * match_table, axis=1)
    expert_loads = jnp.sum(match_table, axis=0)
    return (flat_ids, position, expert_loads)


def shards(tokens, routing, combine, upstream, gate_weight, up_weight, down_weight):
    tok_count = tokens.shape[0]
    top_count = routing.shape[1]
    pick_total = tok_count * top_count
    feature_total = tokens.shape[1]
    hidden_total = gate_weight.shape[2]
    expert_total = lax.axis_size(EXPERT_AXES)
    group_total = lax.axis_size(DP_AXES)
    core_total = lax.axis_size("c")
    capacity = max(tok_count // 2, top_count * tok_count // expert_total + tok_count // 4)
    local_weights = jnp.concatenate([gate_weight[0], up_weight[0], down_weight[0]], axis=1)
    full_weights = lax.all_gather(local_weights, DP_AXES, axis=0, tiled=True)
    gate_full = full_weights[:, :hidden_total]
    up_full = full_weights[:, hidden_total : 2 * hidden_total]
    down_full = full_weights[:, 2 * hidden_total :]
    stacked = full_weights[:, : 2 * hidden_total]
    flat_ids, position, expert_loads = pick_slots(routing, expert_total)
    upstream_wide = upstream.astype(jnp.float32)
    pick_cotangent = (
        (combine[:, :, None] * upstream_wide[:, None, :])
        .reshape(pick_total, feature_total)
        .astype(jnp.bfloat16)
    )
    slot_index = flat_ids * capacity + position
    select = (
        slot_index[None, :] == jnp.arange(expert_total * capacity, dtype=jnp.int32)[:, None]
    ).astype(jnp.bfloat16)
    payload = jnp.concatenate([jnp.repeat(tokens, top_count, axis=0), pick_cotangent], axis=1)
    sending = jnp.dot(select, payload, preferred_element_type=jnp.float32).astype(jnp.bfloat16)
    arrived_both = trade_rows(
        sending.reshape(expert_total, capacity, 2 * feature_total)
    ).reshape(expert_total * capacity, 2 * feature_total)
    arrived = arrived_both[:, :feature_total]
    cot_arrived = arrived_both[:, feature_total:]
    results, gate_pre, up_pre = expert_forward(arrived, stacked, down_full)
    input_grads, deltas = expert_backward(cot_arrived, gate_pre, up_pre, stacked, down_full)
    piece = lax.dot_general(
        arrived, deltas, (((0,), (0,)), ((), ())), preferred_element_type=jnp.float32
    )
    slice_rows = gate_weight.shape[1]
    blocks = piece.reshape(group_total // core_total, core_total, slice_rows, 2 * hidden_total)
    core = lax.axis_index("c")
    own_blocks = lax.dynamic_index_in_dim(blocks, core, axis=1, keepdims=False)
    other_blocks = lax.dynamic_index_in_dim(blocks, 1 - core, axis=1, keepdims=False)
    core_summed = own_blocks + lax.ppermute(other_blocks, "c", perm=[(0, 1), (1, 0)])
    summed = lax.psum_scatter(core_summed, CHIP_AXES, scatter_dimension=0, tiled=True)
    summed = summed.reshape(slice_rows, 2 * hidden_total) / group_total
    row_major = Layout(major_to_minor=(0, 1))
    back = jnp.concatenate(
        [with_layout_constraint(results, row_major), with_layout_constraint(input_grads, row_major)],
        axis=1,
    )
    returned = trade_rows(back.reshape(expert_total, capacity, 2 * feature_total)).reshape(
        expert_total * capacity, 2 * feature_total
    )
    pick_rows = lax.dot_general(
        select,
        returned[:, :feature_total],
        (((0,), (0,)), ((), ())),
        preferred_element_type=jnp.float32,
    )
    token_select = jnp.any(
        slot_index.reshape(tok_count, top_count)[:, :, None]
        == jnp.arange(expert_total * capacity, dtype=jnp.int32)[None, None, :],
        axis=1,
    ).astype(jnp.bfloat16)
    token_grad = jnp.dot(
        token_select, returned[:, feature_total:], preferred_element_type=jnp.float32
    ).astype(jnp.bfloat16)
    gate_grad = summed[:, :hidden_total][None]
    up_grad = summed[:, hidden_total:][None]
    pick_wide = pick_rows.reshape(tok_count, top_count, feature_total)
    layer_output = jnp.sum(combine[:, :, None] * pick_wide, axis=1).astype(jnp.bfloat16)
    combine_grad = jnp.sum(upstream_wide[:, None, :] * pick_wide, axis=2)
    return (layer_output, token_grad, combine_grad, gate_grad, up_grad)


def solution(mesh):
    dp_size = mesh.shape["dp"]
    expert_size = mesh.shape["expert"]
    fine = Mesh(
        mesh.devices.reshape(dp_size // 4, 2, 2, 2, expert_size // 2),
        DP_AXES + EXPERT_AXES,
    )
    placed = (
        P(TOKEN_AXES, None),
        P(TOKEN_AXES, None),
        P(TOKEN_AXES, None),
        P(TOKEN_AXES, None),
        P(EXPERT_AXES, DP_AXES, None),
        P(EXPERT_AXES, DP_AXES, None),
        P(EXPERT_AXES, DP_AXES, None),
    )
    return jax.shard_map(
        shards,
        mesh=fine,
        in_specs=placed,
        out_specs=(
            P(TOKEN_AXES, None),
            P(TOKEN_AXES, None),
            P(TOKEN_AXES, None),
            P(EXPERT_AXES, DP_AXES, None),
            P(EXPERT_AXES, DP_AXES, None),
        ),
        check_vma=False,
    )
```

```python
import jax
import jax.numpy as jnp
from jax import lax
from jax.experimental.layout import Layout, with_layout_constraint
from jax.sharding import Mesh
from jax.sharding import PartitionSpec as P

DP_AXES = ("y", "xl", "c")
CHIP_AXES = ("y", "xl")
EXPERT_AXES = ("xh", "z")
TOKEN_AXES = DP_AXES + EXPERT_AXES


def expert_forward(input_rows, stacked, down_full):
    hidden_total = stacked.shape[1] // 2
    both_pre = jnp.dot(input_rows, stacked, preferred_element_type=jnp.float32)
    gate_pre = both_pre[:, :hidden_total]
    up_pre = both_pre[:, hidden_total:]
    hidden = (jax.nn.silu(gate_pre) * up_pre).astype(jnp.bfloat16)
    results = lax.dot_general(
        hidden, down_full, (((1,), (1,)), ((), ())), preferred_element_type=jnp.float32
    )
    return (results.astype(jnp.bfloat16), gate_pre, up_pre)


def expert_backward(cotangent, gate_pre, up_pre, stacked, down_full):
    hidden_grad = jnp.dot(cotangent, down_full, preferred_element_type=jnp.float32)
    sigmoid_value = jax.nn.sigmoid(gate_pre)
    gate_delta = (
        hidden_grad * up_pre * sigmoid_value * (1.0 + gate_pre * (1.0 - sigmoid_value))
    ).astype(jnp.bfloat16)
    up_delta = (hidden_grad * jax.nn.silu(gate_pre)).astype(jnp.bfloat16)
    deltas = jnp.concatenate([gate_delta, up_delta], axis=1)
    input_grads = lax.dot_general(
        deltas, stacked, (((1,), (1,)), ((), ())), preferred_element_type=jnp.float32
    )
    return (input_grads.astype(jnp.bfloat16), deltas)


def trade_rows(buffer):
    return lax.all_to_all(buffer, EXPERT_AXES, split_axis=0, concat_axis=0, tiled=True)


def pick_slots(routing, expert_total):
    flat_ids = routing.reshape(-1)
    match_table = (flat_ids[:, None] == jnp.arange(expert_total, dtype=jnp.int32)[None, :]).astype(
        jnp.int32
    )
    position = jnp.sum((jnp.cumsum(match_table, axis=0) - 1) * match_table, axis=1)
    expert_loads = jnp.sum(match_table, axis=0)
    return (flat_ids, position, expert_loads)


def shards(tokens, routing, combine, upstream, gate_weight, up_weight, down_weight):
    tok_count = tokens.shape[0]
    top_count = routing.shape[1]
    pick_total = tok_count * top_count
    feature_total = tokens.shape[1]
    hidden_total = gate_weight.shape[2]
    expert_total = lax.axis_size(EXPERT_AXES)
    group_total = lax.axis_size(DP_AXES)
    core_total = lax.axis_size("c")
    capacity = max(tok_count // 2, top_count * tok_count // expert_total + tok_count // 4)
    local_weights = jnp.concatenate([gate_weight[0], up_weight[0], down_weight[0]], axis=1)
    full_weights = lax.all_gather(local_weights, DP_AXES, axis=0, tiled=True)
    gate_full = full_weights[:, :hidden_total]
    up_full = full_weights[:, hidden_total : 2 * hidden_total]
    down_full = full_weights[:, 2 * hidden_total :]
    stacked = full_weights[:, : 2 * hidden_total]
    flat_ids, position, expert_loads = pick_slots(routing, expert_total)
    upstream_wide = upstream.astype(jnp.float32)
    pick_cotangent = (
        (combine[:, :, None] * upstream_wide[:, None, :])
        .reshape(pick_total, feature_total)
        .astype(jnp.bfloat16)
    )
    slot_index = flat_ids * capacity + position
    select = (
        slot_index[None, :] == jnp.arange(expert_total * capacity, dtype=jnp.int32)[:, None]
    ).astype(jnp.bfloat16)
    payload = jnp.concatenate([jnp.repeat(tokens, top_count, axis=0), pick_cotangent], axis=1)
    sending = jnp.dot(select, payload, preferred_element_type=jnp.float32).astype(jnp.bfloat16)
    arrived_both = trade_rows(
        sending.reshape(expert_total, capacity, 2 * feature_total)
    ).reshape(expert_total * capacity, 2 * feature_total)
    arrived = arrived_both[:, :feature_total]
    cot_arrived = arrived_both[:, feature_total:]
    results, gate_pre, up_pre = expert_forward(arrived, stacked, down_full)
    input_grads, deltas = expert_backward(cot_arrived, gate_pre, up_pre, stacked, down_full)
    piece = lax.dot_general(
        arrived, deltas, (((0,), (0,)), ((), ())), preferred_element_type=jnp.float32
    )
    piece, results, input_grads = lax.optimization_barrier((piece, results, input_grads))
    slice_rows = gate_weight.shape[1]
    blocks = piece.reshape(group_total // core_total, core_total, slice_rows, 2 * hidden_total)
    core = lax.axis_index("c")
    own_blocks = lax.dynamic_index_in_dim(blocks, core, axis=1, keepdims=False)
    other_blocks = lax.dynamic_index_in_dim(blocks, 1 - core, axis=1, keepdims=False)
    core_summed = own_blocks + lax.ppermute(other_blocks, "c", perm=[(0, 1), (1, 0)])
    summed = lax.psum_scatter(core_summed, CHIP_AXES, scatter_dimension=0, tiled=True)
    summed = summed.reshape(slice_rows, 2 * hidden_total) / group_total
    row_major = Layout(major_to_minor=(0, 1))
    back = jnp.concatenate(
        [with_layout_constraint(results, row_major), with_layout_constraint(input_grads, row_major)],
        axis=1,
    )
    returned = trade_rows(back.reshape(expert_total, capacity, 2 * feature_total)).reshape(
        expert_total * capacity, 2 * feature_total
    )
    pick_rows = lax.dot_general(
        select,
        returned[:, :feature_total],
        (((0,), (0,)), ((), ())),
        preferred_element_type=jnp.float32,
    )
    token_select = jnp.any(
        slot_index.reshape(tok_count, top_count)[:, :, None]
        == jnp.arange(expert_total * capacity, dtype=jnp.int32)[None, None, :],
        axis=1,
    ).astype(jnp.bfloat16)
    token_grad = jnp.dot(
        token_select, returned[:, feature_total:], preferred_element_type=jnp.float32
    ).astype(jnp.bfloat16)
    pick_wide = pick_rows.reshape(tok_count, top_count, feature_total)
    layer_output = jnp.sum(combine[:, :, None] * pick_wide, axis=1).astype(jnp.bfloat16)
    combine_grad = jnp.sum(upstream_wide[:, None, :] * pick_wide, axis=2)
    after_tokens = summed + 0.0 * layer_output[0, 0].astype(jnp.float32)
    gate_grad = after_tokens[:, :hidden_total][None]
    up_grad = after_tokens[:, hidden_total:][None]
    return (layer_output, token_grad, combine_grad, gate_grad, up_grad)


def solution(mesh):
    dp_size = mesh.shape["dp"]
    expert_size = mesh.shape["expert"]
    fine = Mesh(
        mesh.devices.reshape(dp_size // 4, 2, 2, 2, expert_size // 2),
        DP_AXES + EXPERT_AXES,
    )
    placed = (
        P(TOKEN_AXES, None),
        P(TOKEN_AXES, None),
        P(TOKEN_AXES, None),
        P(TOKEN_AXES, None),
        P(EXPERT_AXES, DP_AXES, None),
        P(EXPERT_AXES, DP_AXES, None),
        P(EXPERT_AXES, DP_AXES, None),
    )
    return jax.shard_map(
        shards,
        mesh=fine,
        in_specs=placed,
        out_specs=(
            P(TOKEN_AXES, None),
            P(TOKEN_AXES, None),
            P(TOKEN_AXES, None),
            P(EXPERT_AXES, DP_AXES, None),
            P(EXPERT_AXES, DP_AXES, None),
        ),
        check_vma=False,
    )
```

```python
import jax
import jax.numpy as jnp
from jax import lax
from jax.experimental.layout import Layout, with_layout_constraint
from jax.sharding import Mesh
from jax.sharding import PartitionSpec as P

DP_AXES = ("y", "xl", "c")
CHIP_AXES = ("y", "xl")
EXPERT_AXES = ("xh", "z")
TOKEN_AXES = DP_AXES + EXPERT_AXES


def expert_forward(input_rows, stacked, down_full):
    hidden_total = stacked.shape[1] // 2
    both_pre = jnp.dot(input_rows, stacked, preferred_element_type=jnp.float32)
    gate_pre = both_pre[:, :hidden_total]
    up_pre = both_pre[:, hidden_total:]
    hidden = (jax.nn.silu(gate_pre) * up_pre).astype(jnp.bfloat16)
    results = lax.dot_general(
        hidden, down_full, (((1,), (1,)), ((), ())), preferred_element_type=jnp.float32
    )
    return (results.astype(jnp.bfloat16), gate_pre, up_pre)


def expert_backward(cotangent, gate_pre, up_pre, stacked, down_full):
    hidden_grad = jnp.dot(cotangent, down_full, preferred_element_type=jnp.float32)
    sigmoid_value = jax.nn.sigmoid(gate_pre)
    gate_delta = (
        hidden_grad * up_pre * sigmoid_value * (1.0 + gate_pre * (1.0 - sigmoid_value))
    ).astype(jnp.bfloat16)
    up_delta = (hidden_grad * jax.nn.silu(gate_pre)).astype(jnp.bfloat16)
    deltas = jnp.concatenate([gate_delta, up_delta], axis=1)
    input_grads = lax.dot_general(
        deltas, stacked, (((1,), (1,)), ((), ())), preferred_element_type=jnp.float32
    )
    return (input_grads.astype(jnp.bfloat16), deltas)


def trade_rows(buffer):
    return lax.all_to_all(buffer, EXPERT_AXES, split_axis=0, concat_axis=0, tiled=True)


def pick_slots(routing, expert_total):
    flat_ids = routing.reshape(-1)
    match_table = (flat_ids[:, None] == jnp.arange(expert_total, dtype=jnp.int32)[None, :]).astype(
        jnp.int32
    )
    position = jnp.sum((jnp.cumsum(match_table, axis=0) - 1) * match_table, axis=1)
    expert_loads = jnp.sum(match_table, axis=0)
    return (flat_ids, position, expert_loads)


def shards(tokens, routing, combine, upstream, gate_weight, up_weight, down_weight):
    tok_count = tokens.shape[0]
    top_count = routing.shape[1]
    pick_total = tok_count * top_count
    feature_total = tokens.shape[1]
    hidden_total = gate_weight.shape[2]
    expert_total = lax.axis_size(EXPERT_AXES)
    group_total = lax.axis_size(DP_AXES)
    core_total = lax.axis_size("c")
    capacity = max(tok_count // 2, top_count * tok_count // expert_total + tok_count // 4)
    local_weights = jnp.concatenate([gate_weight[0], up_weight[0], down_weight[0]], axis=1)
    full_weights = lax.all_gather(local_weights, DP_AXES, axis=0, tiled=True)
    gate_full = full_weights[:, :hidden_total]
    up_full = full_weights[:, hidden_total : 2 * hidden_total]
    down_full = full_weights[:, 2 * hidden_total :]
    stacked = full_weights[:, : 2 * hidden_total]
    flat_ids, position, expert_loads = pick_slots(routing, expert_total)
    upstream_wide = upstream.astype(jnp.float32)
    pick_cotangent = (
        (combine[:, :, None] * upstream_wide[:, None, :])
        .reshape(pick_total, feature_total)
        .astype(jnp.bfloat16)
    )
    slot_index = flat_ids * capacity + position
    select = (
        slot_index[None, :] == jnp.arange(expert_total * capacity, dtype=jnp.int32)[:, None]
    ).astype(jnp.bfloat16)
    payload = jnp.concatenate([jnp.repeat(tokens, top_count, axis=0), pick_cotangent], axis=1)
    sending = jnp.dot(select, payload, preferred_element_type=jnp.float32).astype(jnp.bfloat16)
    arrived_both = trade_rows(
        sending.reshape(expert_total, capacity, 2 * feature_total)
    ).reshape(expert_total * capacity, 2 * feature_total)
    arrived = arrived_both[:, :feature_total]
    cot_arrived = arrived_both[:, feature_total:]
    results, gate_pre, up_pre = expert_forward(arrived, stacked, down_full)
    input_grads, deltas = expert_backward(cot_arrived, gate_pre, up_pre, stacked, down_full)
    piece = lax.dot_general(
        arrived, deltas, (((0,), (0,)), ((), ())), preferred_element_type=jnp.float32
    )
    slice_rows = gate_weight.shape[1]
    blocks = piece.reshape(group_total // core_total, core_total, slice_rows, 2 * hidden_total)
    core = lax.axis_index("c")
    own_blocks = lax.dynamic_index_in_dim(blocks, core, axis=1, keepdims=False)
    other_blocks = lax.dynamic_index_in_dim(blocks, 1 - core, axis=1, keepdims=False)
    core_summed = own_blocks + lax.ppermute(other_blocks, "c", perm=[(0, 1), (1, 0)])
    core_summed, results, input_grads = lax.optimization_barrier((core_summed, results, input_grads))
    summed = lax.psum_scatter(core_summed, CHIP_AXES, scatter_dimension=0, tiled=True)
    summed = summed.reshape(slice_rows, 2 * hidden_total) / group_total
    row_major = Layout(major_to_minor=(0, 1))
    back = jnp.concatenate(
        [with_layout_constraint(results, row_major), with_layout_constraint(input_grads, row_major)],
        axis=1,
    )
    returned = trade_rows(back.reshape(expert_total, capacity, 2 * feature_total)).reshape(
        expert_total * capacity, 2 * feature_total
    )
    pick_rows = lax.dot_general(
        select,
        returned[:, :feature_total],
        (((0,), (0,)), ((), ())),
        preferred_element_type=jnp.float32,
    )
    token_select = jnp.any(
        slot_index.reshape(tok_count, top_count)[:, :, None]
        == jnp.arange(expert_total * capacity, dtype=jnp.int32)[None, None, :],
        axis=1,
    ).astype(jnp.bfloat16)
    token_grad = jnp.dot(
        token_select, returned[:, feature_total:], preferred_element_type=jnp.float32
    ).astype(jnp.bfloat16)
    pick_wide = pick_rows.reshape(tok_count, top_count, feature_total)
    layer_output = jnp.sum(combine[:, :, None] * pick_wide, axis=1).astype(jnp.bfloat16)
    combine_grad = jnp.sum(upstream_wide[:, None, :] * pick_wide, axis=2)
    after_tokens = summed + 0.0 * layer_output[0, 0].astype(jnp.float32)
    gate_grad = after_tokens[:, :hidden_total][None]
    up_grad = after_tokens[:, hidden_total:][None]
    return (layer_output, token_grad, combine_grad, gate_grad, up_grad)


def solution(mesh):
    dp_size = mesh.shape["dp"]
    expert_size = mesh.shape["expert"]
    fine = Mesh(
        mesh.devices.reshape(dp_size // 4, 2, 2, 2, expert_size // 2),
        DP_AXES + EXPERT_AXES,
    )
    placed = (
        P(TOKEN_AXES, None),
        P(TOKEN_AXES, None),
        P(TOKEN_AXES, None),
        P(TOKEN_AXES, None),
        P(EXPERT_AXES, DP_AXES, None),
        P(EXPERT_AXES, DP_AXES, None),
        P(EXPERT_AXES, DP_AXES, None),
    )
    return jax.shard_map(
        shards,
        mesh=fine,
        in_specs=placed,
        out_specs=(
            P(TOKEN_AXES, None),
            P(TOKEN_AXES, None),
            P(TOKEN_AXES, None),
            P(EXPERT_AXES, DP_AXES, None),
            P(EXPERT_AXES, DP_AXES, None),
        ),
        check_vma=False,
    )
```

```python
import jax
import jax.numpy as jnp
from jax import lax
from jax.experimental.layout import Layout, with_layout_constraint
from jax.sharding import Mesh
from jax.sharding import PartitionSpec as P

DP_AXES = ("y", "xl", "c")
CHIP_AXES = ("y", "xl")
EXPERT_AXES = ("xh", "z")
TOKEN_AXES = DP_AXES + EXPERT_AXES


def expert_forward(input_rows, stacked, down_full):
    hidden_total = stacked.shape[1] // 2
    both_pre = jnp.dot(input_rows, stacked, preferred_element_type=jnp.float32)
    gate_pre = both_pre[:, :hidden_total]
    up_pre = both_pre[:, hidden_total:]
    hidden = (jax.nn.silu(gate_pre) * up_pre).astype(jnp.bfloat16)
    results = lax.dot_general(
        hidden, down_full, (((1,), (1,)), ((), ())), preferred_element_type=jnp.float32
    )
    return (results.astype(jnp.bfloat16), gate_pre, up_pre)


def expert_backward(cotangent, gate_pre, up_pre, stacked, down_full):
    hidden_grad = jnp.dot(cotangent, down_full, preferred_element_type=jnp.float32)
    sigmoid_value = jax.nn.sigmoid(gate_pre)
    gate_delta = (
        hidden_grad * up_pre * sigmoid_value * (1.0 + gate_pre * (1.0 - sigmoid_value))
    ).astype(jnp.bfloat16)
    up_delta = (hidden_grad * jax.nn.silu(gate_pre)).astype(jnp.bfloat16)
    deltas = jnp.concatenate([gate_delta, up_delta], axis=1)
    input_grads = lax.dot_general(
        deltas, stacked, (((1,), (1,)), ((), ())), preferred_element_type=jnp.float32
    )
    return (input_grads.astype(jnp.bfloat16), deltas)


def trade_rows(buffer):
    return lax.all_to_all(buffer, EXPERT_AXES, split_axis=0, concat_axis=0, tiled=True)


def pick_slots(routing, expert_total):
    flat_ids = routing.reshape(-1)
    match_table = (flat_ids[:, None] == jnp.arange(expert_total, dtype=jnp.int32)[None, :]).astype(
        jnp.int32
    )
    position = jnp.sum((jnp.cumsum(match_table, axis=0) - 1) * match_table, axis=1)
    expert_loads = jnp.sum(match_table, axis=0)
    return (flat_ids, position, expert_loads)


def shards(tokens, routing, combine, upstream, gate_weight, up_weight, down_weight):
    tok_count = tokens.shape[0]
    top_count = routing.shape[1]
    pick_total = tok_count * top_count
    feature_total = tokens.shape[1]
    hidden_total = gate_weight.shape[2]
    expert_total = lax.axis_size(EXPERT_AXES)
    group_total = lax.axis_size(DP_AXES)
    core_total = lax.axis_size("c")
    capacity = max(tok_count // 2, top_count * tok_count // expert_total + tok_count // 4)
    local_weights = jnp.concatenate([gate_weight[0], up_weight[0], down_weight[0]], axis=1)
    full_weights = lax.all_gather(local_weights, DP_AXES, axis=0, tiled=True)
    gate_full = full_weights[:, :hidden_total]
    up_full = full_weights[:, hidden_total : 2 * hidden_total]
    down_full = full_weights[:, 2 * hidden_total :]
    stacked = full_weights[:, : 2 * hidden_total]
    flat_ids, position, expert_loads = pick_slots(routing, expert_total)
    upstream_wide = upstream.astype(jnp.float32)
    pick_cotangent = (
        (combine[:, :, None] * upstream_wide[:, None, :])
        .reshape(pick_total, feature_total)
        .astype(jnp.bfloat16)
    )
    slot_index = flat_ids * capacity + position
    select = (
        slot_index[None, :] == jnp.arange(expert_total * capacity, dtype=jnp.int32)[:, None]
    ).astype(jnp.bfloat16)
    payload = jnp.concatenate([jnp.repeat(tokens, top_count, axis=0), pick_cotangent], axis=1)
    sending = jnp.dot(select, payload, preferred_element_type=jnp.float32).astype(jnp.bfloat16)
    arrived_both = trade_rows(
        sending.reshape(expert_total, capacity, 2 * feature_total)
    ).reshape(expert_total * capacity, 2 * feature_total)
    arrived = arrived_both[:, :feature_total]
    cot_arrived = arrived_both[:, feature_total:]
    results, gate_pre, up_pre = expert_forward(arrived, stacked, down_full)
    input_grads, deltas = expert_backward(cot_arrived, gate_pre, up_pre, stacked, down_full)
    piece = lax.dot_general(
        arrived, deltas, (((0,), (0,)), ((), ())), preferred_element_type=jnp.float32
    )
    slice_rows = gate_weight.shape[1]
    blocks = piece.reshape(group_total // core_total, core_total, slice_rows, 2 * hidden_total)
    core = lax.axis_index("c")
    own_blocks = lax.dynamic_index_in_dim(blocks, core, axis=1, keepdims=False)
    other_blocks = lax.dynamic_index_in_dim(blocks, 1 - core, axis=1, keepdims=False)
    core_summed = own_blocks + lax.ppermute(other_blocks, "c", perm=[(0, 1), (1, 0)])
    summed = lax.psum_scatter(core_summed, CHIP_AXES, scatter_dimension=0, tiled=True)
    summed = summed.reshape(slice_rows, 2 * hidden_total) / group_total
    row_major = Layout(major_to_minor=(0, 1))
    back = jnp.concatenate(
        [with_layout_constraint(results, row_major), with_layout_constraint(input_grads, row_major)],
        axis=1,
    )
    returned = trade_rows(back.reshape(expert_total, capacity, 2 * feature_total)).reshape(
        expert_total * capacity, 2 * feature_total
    )
    pick_rows = lax.dot_general(
        select,
        returned[:, :feature_total],
        (((0,), (0,)), ((), ())),
        preferred_element_type=jnp.float32,
    )
    token_select = jnp.any(
        slot_index.reshape(tok_count, top_count)[:, :, None]
        == jnp.arange(expert_total * capacity, dtype=jnp.int32)[None, None, :],
        axis=1,
    ).astype(jnp.bfloat16)
    token_grad = jnp.dot(
        token_select, returned[:, feature_total:], preferred_element_type=jnp.float32
    ).astype(jnp.bfloat16)
    pick_wide = pick_rows.reshape(tok_count, top_count, feature_total)
    layer_output = jnp.sum(combine[:, :, None] * pick_wide, axis=1).astype(jnp.bfloat16)
    combine_grad = jnp.sum(upstream_wide[:, None, :] * pick_wide, axis=2)
    after_tokens = summed + 0.0 * layer_output[0, 0].astype(jnp.float32)
    gate_grad = after_tokens[:, :hidden_total][None]
    up_grad = after_tokens[:, hidden_total:][None]
    return (layer_output, token_grad, combine_grad, gate_grad, up_grad)


def solution(mesh):
    dp_size = mesh.shape["dp"]
    expert_size = mesh.shape["expert"]
    fine = Mesh(
        mesh.devices.reshape(dp_size // 4, 2, 2, 2, expert_size // 2),
        DP_AXES + EXPERT_AXES,
    )
    placed = (
        P(TOKEN_AXES, None),
        P(TOKEN_AXES, None),
        P(TOKEN_AXES, None),
        P(TOKEN_AXES, None),
        P(EXPERT_AXES, DP_AXES, None),
        P(EXPERT_AXES, DP_AXES, None),
        P(EXPERT_AXES, DP_AXES, None),
    )
    return jax.shard_map(
        shards,
        mesh=fine,
        in_specs=placed,
        out_specs=(
            P(TOKEN_AXES, None),
            P(TOKEN_AXES, None),
            P(TOKEN_AXES, None),
            P(EXPERT_AXES, DP_AXES, None),
            P(EXPERT_AXES, DP_AXES, None),
        ),
        check_vma=False,
    )
```

```python
import jax
import jax.numpy as jnp
from jax import lax
from jax.experimental.layout import Layout, with_layout_constraint
from jax.sharding import Mesh
from jax.sharding import PartitionSpec as P

DP_AXES = ("y", "xl", "c")
CHIP_AXES = ("y", "xl")
EXPERT_AXES = ("xh", "z")
TOKEN_AXES = DP_AXES + EXPERT_AXES


def expert_forward(input_rows, stacked, down_full):
    hidden_total = stacked.shape[1] // 2
    both_pre = jnp.dot(input_rows, stacked, preferred_element_type=jnp.float32)
    gate_pre = both_pre[:, :hidden_total]
    up_pre = both_pre[:, hidden_total:]
    hidden = (jax.nn.silu(gate_pre) * up_pre).astype(jnp.bfloat16)
    results = lax.dot_general(
        hidden, down_full, (((1,), (1,)), ((), ())), preferred_element_type=jnp.float32
    )
    return (results.astype(jnp.bfloat16), gate_pre, up_pre)


def expert_backward(cotangent, gate_pre, up_pre, stacked, down_full):
    hidden_grad = jnp.dot(cotangent, down_full, preferred_element_type=jnp.float32)
    sigmoid_value = jax.nn.sigmoid(gate_pre)
    gate_delta = (
        hidden_grad * up_pre * sigmoid_value * (1.0 + gate_pre * (1.0 - sigmoid_value))
    ).astype(jnp.bfloat16)
    up_delta = (hidden_grad * jax.nn.silu(gate_pre)).astype(jnp.bfloat16)
    deltas = jnp.concatenate([gate_delta, up_delta], axis=1)
    input_grads = lax.dot_general(
        deltas, stacked, (((1,), (1,)), ((), ())), preferred_element_type=jnp.float32
    )
    return (input_grads.astype(jnp.bfloat16), deltas)


def swap_partner(values, axis):
    return lax.ppermute(values, axis, perm=[(0, 1), (1, 0)])


def ring_gather(values, axis, size):
    me = lax.axis_index(axis)
    held = [values]
    moving = values
    for _ in range(size - 1):
        moving = lax.ppermute(moving, axis, perm=[(i, (i + 1) % size) for i in range(size)])
        held.append(moving)
    stacked = jnp.stack(held)
    order = (me - jnp.arange(size, dtype=jnp.int32)) % size
    return jnp.take(stacked, order, axis=0)


def ring_reduce_scatter(blocks, axis, size):
    me = lax.axis_index(axis)
    carry = lax.dynamic_index_in_dim(blocks, (me - 1) % size, axis=0, keepdims=False)
    for hop in range(size - 1):
        arrived = lax.ppermute(carry, axis, perm=[(i, (i + 1) % size) for i in range(size)])
        own = lax.dynamic_index_in_dim(blocks, (me - hop - 2) % size, axis=0, keepdims=False)
        carry = arrived + own
    return carry


def ordered_pair(own, other, axis):
    first = lax.axis_index(axis) == 0
    return jnp.stack([jnp.where(first, own, other), jnp.where(first, other, own)])


def trade_rows(buffer):
    return lax.all_to_all(buffer, EXPERT_AXES, split_axis=0, concat_axis=0, tiled=True)


def pick_slots(routing, expert_total):
    flat_ids = routing.reshape(-1)
    match_table = (flat_ids[:, None] == jnp.arange(expert_total, dtype=jnp.int32)[None, :]).astype(
        jnp.int32
    )
    position = jnp.sum((jnp.cumsum(match_table, axis=0) - 1) * match_table, axis=1)
    expert_loads = jnp.sum(match_table, axis=0)
    return (flat_ids, position, expert_loads)


def shards(tokens, routing, combine, upstream, gate_weight, up_weight, down_weight):
    tok_count = tokens.shape[0]
    top_count = routing.shape[1]
    pick_total = tok_count * top_count
    feature_total = tokens.shape[1]
    hidden_total = gate_weight.shape[2]
    expert_total = lax.axis_size(EXPERT_AXES)
    group_total = lax.axis_size(DP_AXES)
    core_total = lax.axis_size("c")
    capacity = max(tok_count // 2, top_count * tok_count // expert_total + tok_count // 4)
    local_weights = jnp.concatenate([gate_weight[0], up_weight[0], down_weight[0]], axis=1)
    y_size = lax.axis_size("y")
    along_y = ring_gather(local_weights, "y", y_size)
    along_xl = ordered_pair(along_y, swap_partner(along_y, "xl"), "xl")
    along_c = ordered_pair(along_xl, swap_partner(along_xl, "c"), "c")
    full_weights = jnp.transpose(along_c, (2, 1, 0, 3, 4)).reshape(-1, local_weights.shape[1])
    gate_full = full_weights[:, :hidden_total]
    up_full = full_weights[:, hidden_total : 2 * hidden_total]
    down_full = full_weights[:, 2 * hidden_total :]
    stacked = full_weights[:, : 2 * hidden_total]
    flat_ids, position, expert_loads = pick_slots(routing, expert_total)
    upstream_wide = upstream.astype(jnp.float32)
    pick_cotangent = (
        (combine[:, :, None] * upstream_wide[:, None, :])
        .reshape(pick_total, feature_total)
        .astype(jnp.bfloat16)
    )
    slot_index = flat_ids * capacity + position
    select = (
        slot_index[None, :] == jnp.arange(expert_total * capacity, dtype=jnp.int32)[:, None]
    ).astype(jnp.bfloat16)
    payload = jnp.concatenate([jnp.repeat(tokens, top_count, axis=0), pick_cotangent], axis=1)
    sending = jnp.dot(select, payload, preferred_element_type=jnp.float32).astype(jnp.bfloat16)
    arrived_both = trade_rows(
        sending.reshape(expert_total, capacity, 2 * feature_total)
    ).reshape(expert_total * capacity, 2 * feature_total)
    arrived = arrived_both[:, :feature_total]
    cot_arrived = arrived_both[:, feature_total:]
    results, gate_pre, up_pre = expert_forward(arrived, stacked, down_full)
    input_grads, deltas = expert_backward(cot_arrived, gate_pre, up_pre, stacked, down_full)
    piece = lax.dot_general(
        arrived, deltas, (((0,), (0,)), ((), ())), preferred_element_type=jnp.float32
    )
    slice_rows = gate_weight.shape[1]
    blocks = piece.reshape(group_total // core_total, core_total, slice_rows, 2 * hidden_total)
    core = lax.axis_index("c")
    own_blocks = lax.dynamic_index_in_dim(blocks, core, axis=1, keepdims=False)
    other_blocks = lax.dynamic_index_in_dim(blocks, 1 - core, axis=1, keepdims=False)
    core_summed = own_blocks + lax.ppermute(other_blocks, "c", perm=[(0, 1), (1, 0)])
    by_xl = core_summed.reshape(y_size, lax.axis_size("xl"), slice_rows, 2 * hidden_total)
    xl = lax.axis_index("xl")
    keep_xl = lax.dynamic_index_in_dim(by_xl, xl, axis=1, keepdims=False)
    send_xl = lax.dynamic_index_in_dim(by_xl, 1 - xl, axis=1, keepdims=False)
    xl_summed = keep_xl + swap_partner(send_xl, "xl")
    summed = ring_reduce_scatter(xl_summed, "y", y_size)
    summed = summed.reshape(slice_rows, 2 * hidden_total) / group_total
    row_major = Layout(major_to_minor=(0, 1))
    back = jnp.concatenate(
        [with_layout_constraint(results, row_major), with_layout_constraint(input_grads, row_major)],
        axis=1,
    )
    returned = trade_rows(back.reshape(expert_total, capacity, 2 * feature_total)).reshape(
        expert_total * capacity, 2 * feature_total
    )
    pick_rows = lax.dot_general(
        select,
        returned[:, :feature_total],
        (((0,), (0,)), ((), ())),
        preferred_element_type=jnp.float32,
    )
    token_select = jnp.any(
        slot_index.reshape(tok_count, top_count)[:, :, None]
        == jnp.arange(expert_total * capacity, dtype=jnp.int32)[None, None, :],
        axis=1,
    ).astype(jnp.bfloat16)
    token_grad = jnp.dot(
        token_select, returned[:, feature_total:], preferred_element_type=jnp.float32
    ).astype(jnp.bfloat16)
    pick_wide = pick_rows.reshape(tok_count, top_count, feature_total)
    layer_output = jnp.sum(combine[:, :, None] * pick_wide, axis=1).astype(jnp.bfloat16)
    combine_grad = jnp.sum(upstream_wide[:, None, :] * pick_wide, axis=2)
    after_tokens = summed + 0.0 * layer_output[0, 0].astype(jnp.float32)
    gate_grad = after_tokens[:, :hidden_total][None]
    up_grad = after_tokens[:, hidden_total:][None]
    return (layer_output, token_grad, combine_grad, gate_grad, up_grad)


def solution(mesh):
    dp_size = mesh.shape["dp"]
    expert_size = mesh.shape["expert"]
    fine = Mesh(
        mesh.devices.reshape(dp_size // 4, 2, 2, 2, expert_size // 2),
        DP_AXES + EXPERT_AXES,
    )
    placed = (
        P(TOKEN_AXES, None),
        P(TOKEN_AXES, None),
        P(TOKEN_AXES, None),
        P(TOKEN_AXES, None),
        P(EXPERT_AXES, DP_AXES, None),
        P(EXPERT_AXES, DP_AXES, None),
        P(EXPERT_AXES, DP_AXES, None),
    )
    return jax.shard_map(
        shards,
        mesh=fine,
        in_specs=placed,
        out_specs=(
            P(TOKEN_AXES, None),
            P(TOKEN_AXES, None),
            P(TOKEN_AXES, None),
            P(EXPERT_AXES, DP_AXES, None),
            P(EXPERT_AXES, DP_AXES, None),
        ),
        check_vma=False,
    )
```

```python
import jax
import jax.numpy as jnp
from jax import lax
from jax.experimental.layout import Layout, with_layout_constraint
from jax.sharding import Mesh
from jax.sharding import PartitionSpec as P

DP_AXES = ("y", "xl", "c")
CHIP_AXES = ("y", "xl")
EXPERT_AXES = ("xh", "z")
TRADE_AXES = ("z", "xh")
TOKEN_AXES = DP_AXES + EXPERT_AXES


def expert_forward(input_rows, stacked, down_full):
    hidden_total = stacked.shape[1] // 2
    both_pre = jnp.dot(input_rows, stacked, preferred_element_type=jnp.float32)
    gate_pre = both_pre[:, :hidden_total]
    up_pre = both_pre[:, hidden_total:]
    hidden = (jax.nn.silu(gate_pre) * up_pre).astype(jnp.bfloat16)
    results = lax.dot_general(
        hidden, down_full, (((1,), (1,)), ((), ())), preferred_element_type=jnp.float32
    )
    return (results.astype(jnp.bfloat16), gate_pre, up_pre)


def expert_backward(cotangent, gate_pre, up_pre, stacked, down_full):
    hidden_grad = jnp.dot(cotangent, down_full, preferred_element_type=jnp.float32)
    sigmoid_value = jax.nn.sigmoid(gate_pre)
    gate_delta = (
        hidden_grad * up_pre * sigmoid_value * (1.0 + gate_pre * (1.0 - sigmoid_value))
    ).astype(jnp.bfloat16)
    up_delta = (hidden_grad * jax.nn.silu(gate_pre)).astype(jnp.bfloat16)
    deltas = jnp.concatenate([gate_delta, up_delta], axis=1)
    input_grads = lax.dot_general(
        deltas, stacked, (((1,), (1,)), ((), ())), preferred_element_type=jnp.float32
    )
    return (input_grads.astype(jnp.bfloat16), deltas)


def swap_partner(values, axis):
    return lax.ppermute(values, axis, perm=[(0, 1), (1, 0)])


def ring_gather(values, axis, size):
    me = lax.axis_index(axis)
    held = [values]
    moving = values
    for _ in range(size - 1):
        moving = lax.ppermute(moving, axis, perm=[(i, (i + 1) % size) for i in range(size)])
        held.append(moving)
    stacked = jnp.stack(held)
    order = (me - jnp.arange(size, dtype=jnp.int32)) % size
    return jnp.take(stacked, order, axis=0)


def ring_reduce_scatter(blocks, axis, size):
    me = lax.axis_index(axis)
    carry = lax.dynamic_index_in_dim(blocks, (me - 1) % size, axis=0, keepdims=False)
    for hop in range(size - 1):
        arrived = lax.ppermute(carry, axis, perm=[(i, (i + 1) % size) for i in range(size)])
        own = lax.dynamic_index_in_dim(blocks, (me - hop - 2) % size, axis=0, keepdims=False)
        carry = arrived + own
    return carry


def ordered_pair(own, other, axis):
    first = lax.axis_index(axis) == 0
    return jnp.stack([jnp.where(first, own, other), jnp.where(first, other, own)])


def trade_rows(buffer):
    return lax.all_to_all(buffer, TRADE_AXES, split_axis=0, concat_axis=0, tiled=True)


def pick_slots(routing, expert_total):
    flat_ids = routing.reshape(-1)
    match_table = (flat_ids[:, None] == jnp.arange(expert_total, dtype=jnp.int32)[None, :]).astype(
        jnp.int32
    )
    position = jnp.sum((jnp.cumsum(match_table, axis=0) - 1) * match_table, axis=1)
    expert_loads = jnp.sum(match_table, axis=0)
    return (flat_ids, position, expert_loads)


def shards(tokens, routing, combine, upstream, gate_weight, up_weight, down_weight):
    tok_count = tokens.shape[0]
    top_count = routing.shape[1]
    pick_total = tok_count * top_count
    feature_total = tokens.shape[1]
    hidden_total = gate_weight.shape[2]
    expert_total = lax.axis_size(EXPERT_AXES)
    group_total = lax.axis_size(DP_AXES)
    core_total = lax.axis_size("c")
    capacity = max(tok_count // 2, top_count * tok_count // expert_total + tok_count // 4)
    local_weights = jnp.concatenate([gate_weight[0], up_weight[0], down_weight[0]], axis=1)
    y_size = lax.axis_size("y")
    along_y = ring_gather(local_weights, "y", y_size)
    along_xl = ordered_pair(along_y, swap_partner(along_y, "xl"), "xl")
    along_c = ordered_pair(along_xl, swap_partner(along_xl, "c"), "c")
    full_weights = jnp.transpose(along_c, (2, 1, 0, 3, 4)).reshape(-1, local_weights.shape[1])
    gate_full = full_weights[:, :hidden_total]
    up_full = full_weights[:, hidden_total : 2 * hidden_total]
    down_full = full_weights[:, 2 * hidden_total :]
    stacked = full_weights[:, : 2 * hidden_total]
    flat_ids, position, expert_loads = pick_slots(routing, expert_total)
    upstream_wide = upstream.astype(jnp.float32)
    pick_cotangent = (
        (combine[:, :, None] * upstream_wide[:, None, :])
        .reshape(pick_total, feature_total)
        .astype(jnp.bfloat16)
    )
    z_total = lax.axis_size("z")
    chunk_of = (flat_ids % z_total) * (expert_total // z_total) + flat_ids // z_total
    slot_index = chunk_of * capacity + position
    select = (
        slot_index[None, :] == jnp.arange(expert_total * capacity, dtype=jnp.int32)[:, None]
    ).astype(jnp.bfloat16)
    payload = jnp.concatenate([jnp.repeat(tokens, top_count, axis=0), pick_cotangent], axis=1)
    sending = jnp.dot(select, payload, preferred_element_type=jnp.float32).astype(jnp.bfloat16)
    arrived_both = trade_rows(
        sending.reshape(expert_total, capacity, 2 * feature_total)
    ).reshape(expert_total * capacity, 2 * feature_total)
    arrived = arrived_both[:, :feature_total]
    cot_arrived = arrived_both[:, feature_total:]
    results, gate_pre, up_pre = expert_forward(arrived, stacked, down_full)
    input_grads, deltas = expert_backward(cot_arrived, gate_pre, up_pre, stacked, down_full)
    piece = lax.dot_general(
        arrived, deltas, (((0,), (0,)), ((), ())), preferred_element_type=jnp.float32
    )
    slice_rows = gate_weight.shape[1]
    blocks = piece.reshape(group_total // core_total, core_total, slice_rows, 2 * hidden_total)
    core = lax.axis_index("c")
    own_blocks = lax.dynamic_index_in_dim(blocks, core, axis=1, keepdims=False)
    other_blocks = lax.dynamic_index_in_dim(blocks, 1 - core, axis=1, keepdims=False)
    core_summed = own_blocks + lax.ppermute(other_blocks, "c", perm=[(0, 1), (1, 0)])
    by_xl = core_summed.reshape(y_size, lax.axis_size("xl"), slice_rows, 2 * hidden_total)
    xl = lax.axis_index("xl")
    keep_xl = lax.dynamic_index_in_dim(by_xl, xl, axis=1, keepdims=False)
    send_xl = lax.dynamic_index_in_dim(by_xl, 1 - xl, axis=1, keepdims=False)
    xl_summed = keep_xl + swap_partner(send_xl, "xl")
    summed = ring_reduce_scatter(xl_summed, "y", y_size)
    summed = summed.reshape(slice_rows, 2 * hidden_total) / group_total
    row_major = Layout(major_to_minor=(0, 1))
    back = jnp.concatenate(
        [with_layout_constraint(results, row_major), with_layout_constraint(input_grads, row_major)],
        axis=1,
    )
    returned = trade_rows(back.reshape(expert_total, capacity, 2 * feature_total)).reshape(
        expert_total * capacity, 2 * feature_total
    )
    pick_rows = lax.dot_general(
        select,
        returned[:, :feature_total],
        (((0,), (0,)), ((), ())),
        preferred_element_type=jnp.float32,
    )
    token_select = jnp.any(
        slot_index.reshape(tok_count, top_count)[:, :, None]
        == jnp.arange(expert_total * capacity, dtype=jnp.int32)[None, None, :],
        axis=1,
    ).astype(jnp.bfloat16)
    token_grad = jnp.dot(
        token_select, returned[:, feature_total:], preferred_element_type=jnp.float32
    ).astype(jnp.bfloat16)
    pick_wide = pick_rows.reshape(tok_count, top_count, feature_total)
    layer_output = jnp.sum(combine[:, :, None] * pick_wide, axis=1).astype(jnp.bfloat16)
    combine_grad = jnp.sum(upstream_wide[:, None, :] * pick_wide, axis=2)
    after_tokens = summed + 0.0 * layer_output[0, 0].astype(jnp.float32)
    gate_grad = after_tokens[:, :hidden_total][None]
    up_grad = after_tokens[:, hidden_total:][None]
    return (layer_output, token_grad, combine_grad, gate_grad, up_grad)


def solution(mesh):
    dp_size = mesh.shape["dp"]
    expert_size = mesh.shape["expert"]
    fine = Mesh(
        mesh.devices.reshape(dp_size // 4, 2, 2, 2, expert_size // 2),
        DP_AXES + EXPERT_AXES,
    )
    placed = (
        P(TOKEN_AXES, None),
        P(TOKEN_AXES, None),
        P(TOKEN_AXES, None),
        P(TOKEN_AXES, None),
        P(EXPERT_AXES, DP_AXES, None),
        P(EXPERT_AXES, DP_AXES, None),
        P(EXPERT_AXES, DP_AXES, None),
    )
    return jax.shard_map(
        shards,
        mesh=fine,
        in_specs=placed,
        out_specs=(
            P(TOKEN_AXES, None),
            P(TOKEN_AXES, None),
            P(TOKEN_AXES, None),
            P(EXPERT_AXES, DP_AXES, None),
            P(EXPERT_AXES, DP_AXES, None),
        ),
        check_vma=False,
    )
```

```python
import jax
import jax.numpy as jnp
from jax import lax
from jax.experimental.layout import Layout, with_layout_constraint
from jax.sharding import Mesh
from jax.sharding import PartitionSpec as P

DP_AXES = ("y", "xl", "c")
CHIP_AXES = ("y", "xl")
EXPERT_AXES = ("xh", "z")
TOKEN_AXES = DP_AXES + EXPERT_AXES


def expert_forward(input_rows, stacked, down_full):
    hidden_total = stacked.shape[1] // 2
    both_pre = jnp.dot(input_rows, stacked, preferred_element_type=jnp.float32)
    gate_pre = both_pre[:, :hidden_total]
    up_pre = both_pre[:, hidden_total:]
    hidden = (jax.nn.silu(gate_pre) * up_pre).astype(jnp.bfloat16)
    results = lax.dot_general(
        hidden, down_full, (((1,), (1,)), ((), ())), preferred_element_type=jnp.float32
    )
    return (results.astype(jnp.bfloat16), gate_pre, up_pre)


def expert_backward(cotangent, gate_pre, up_pre, stacked, down_full):
    hidden_grad = jnp.dot(cotangent, down_full, preferred_element_type=jnp.float32)
    sigmoid_value = jax.nn.sigmoid(gate_pre)
    gate_delta = (
        hidden_grad * up_pre * sigmoid_value * (1.0 + gate_pre * (1.0 - sigmoid_value))
    ).astype(jnp.bfloat16)
    up_delta = (hidden_grad * jax.nn.silu(gate_pre)).astype(jnp.bfloat16)
    deltas = jnp.concatenate([gate_delta, up_delta], axis=1)
    input_grads = lax.dot_general(
        deltas, stacked, (((1,), (1,)), ((), ())), preferred_element_type=jnp.float32
    )
    return (input_grads.astype(jnp.bfloat16), deltas)


def swap_partner(values, axis):
    return lax.ppermute(values, axis, perm=[(0, 1), (1, 0)])


def ring_gather(values, axis, size):
    me = lax.axis_index(axis)
    held = [values]
    moving = values
    for _ in range(size - 1):
        moving = lax.ppermute(moving, axis, perm=[(i, (i + 1) % size) for i in range(size)])
        held.append(moving)
    stacked = jnp.stack(held)
    order = (me - jnp.arange(size, dtype=jnp.int32)) % size
    return jnp.take(stacked, order, axis=0)


def ring_reduce_scatter(blocks, axis, size):
    me = lax.axis_index(axis)
    carry = lax.dynamic_index_in_dim(blocks, (me - 1) % size, axis=0, keepdims=False)
    for hop in range(size - 1):
        arrived = lax.ppermute(carry, axis, perm=[(i, (i + 1) % size) for i in range(size)])
        own = lax.dynamic_index_in_dim(blocks, (me - hop - 2) % size, axis=0, keepdims=False)
        carry = arrived + own
    return carry


def ordered_pair(own, other, axis):
    first = lax.axis_index(axis) == 0
    return jnp.stack([jnp.where(first, own, other), jnp.where(first, other, own)])


def trade_rows(buffer):
    return lax.all_to_all(buffer, EXPERT_AXES, split_axis=0, concat_axis=0, tiled=True)


def pick_slots(routing, expert_total):
    flat_ids = routing.reshape(-1)
    match_table = (flat_ids[:, None] == jnp.arange(expert_total, dtype=jnp.int32)[None, :]).astype(
        jnp.int32
    )
    position = jnp.sum((jnp.cumsum(match_table, axis=0) - 1) * match_table, axis=1)
    expert_loads = jnp.sum(match_table, axis=0)
    return (flat_ids, position, expert_loads)


def shards(tokens, routing, combine, upstream, gate_weight, up_weight, down_weight):
    tok_count = tokens.shape[0]
    top_count = routing.shape[1]
    pick_total = tok_count * top_count
    feature_total = tokens.shape[1]
    hidden_total = gate_weight.shape[2]
    expert_total = lax.axis_size(EXPERT_AXES)
    group_total = lax.axis_size(DP_AXES)
    core_total = lax.axis_size("c")
    capacity = max(tok_count // 2, top_count * tok_count // expert_total + tok_count // 4)
    local_weights = jnp.concatenate([gate_weight[0], up_weight[0], down_weight[0]], axis=1)
    y_size = lax.axis_size("y")
    along_y = ring_gather(local_weights, "y", y_size)
    along_xl = ordered_pair(along_y, swap_partner(along_y, "xl"), "xl")
    along_c = ordered_pair(along_xl, swap_partner(along_xl, "c"), "c")
    full_weights = jnp.transpose(along_c, (2, 1, 0, 3, 4)).reshape(-1, local_weights.shape[1])
    gate_full = full_weights[:, :hidden_total]
    up_full = full_weights[:, hidden_total : 2 * hidden_total]
    down_full = full_weights[:, 2 * hidden_total :]
    stacked = full_weights[:, : 2 * hidden_total]
    flat_ids, position, expert_loads = pick_slots(routing, expert_total)
    upstream_wide = upstream.astype(jnp.float32)
    pick_cotangent = (
        (combine[:, :, None] * upstream_wide[:, None, :])
        .reshape(pick_total, feature_total)
        .astype(jnp.bfloat16)
    )
    slot_index = flat_ids * capacity + position
    select = (
        slot_index[None, :] == jnp.arange(expert_total * capacity, dtype=jnp.int32)[:, None]
    ).astype(jnp.bfloat16)
    payload = jnp.concatenate([jnp.repeat(tokens, top_count, axis=0), pick_cotangent], axis=1)
    sending = jnp.dot(select, payload, preferred_element_type=jnp.float32).astype(jnp.bfloat16)
    arrived_both = trade_rows(
        sending.reshape(expert_total, capacity, 2 * feature_total)
    ).reshape(expert_total * capacity, 2 * feature_total)
    arrived = arrived_both[:, :feature_total]
    cot_arrived = arrived_both[:, feature_total:]
    results, gate_pre, up_pre = expert_forward(arrived, stacked, down_full)
    input_grads, deltas = expert_backward(cot_arrived, gate_pre, up_pre, stacked, down_full)
    piece = lax.dot_general(
        arrived, deltas, (((0,), (0,)), ((), ())), preferred_element_type=jnp.float32
    )
    slice_rows = gate_weight.shape[1]
    blocks = piece.reshape(group_total // core_total, core_total, slice_rows, 2 * hidden_total)
    core = lax.axis_index("c")
    own_blocks = lax.dynamic_index_in_dim(blocks, core, axis=1, keepdims=False)
    other_blocks = lax.dynamic_index_in_dim(blocks, 1 - core, axis=1, keepdims=False)
    core_summed = own_blocks + lax.ppermute(other_blocks, "c", perm=[(0, 1), (1, 0)])
    by_xl = core_summed.reshape(y_size, lax.axis_size("xl"), slice_rows, 2 * hidden_total)
    xl = lax.axis_index("xl")
    keep_xl = lax.dynamic_index_in_dim(by_xl, xl, axis=1, keepdims=False)
    send_xl = lax.dynamic_index_in_dim(by_xl, 1 - xl, axis=1, keepdims=False)
    xl_summed = keep_xl + swap_partner(send_xl, "xl")
    summed = ring_reduce_scatter(xl_summed, "y", y_size)
    summed = summed.reshape(slice_rows, 2 * hidden_total) / group_total
    row_major = Layout(major_to_minor=(0, 1))
    returned_out = trade_rows(
        with_layout_constraint(results, row_major).reshape(expert_total, capacity, feature_total)
    ).reshape(expert_total * capacity, feature_total)
    returned_grads = trade_rows(
        with_layout_constraint(input_grads, row_major).reshape(expert_total, capacity, feature_total)
    ).reshape(expert_total * capacity, feature_total)
    pick_rows = lax.dot_general(
        select,
        returned_out,
        (((0,), (0,)), ((), ())),
        preferred_element_type=jnp.float32,
    )
    token_select = jnp.any(
        slot_index.reshape(tok_count, top_count)[:, :, None]
        == jnp.arange(expert_total * capacity, dtype=jnp.int32)[None, None, :],
        axis=1,
    ).astype(jnp.bfloat16)
    token_grad = jnp.dot(
        token_select, returned_grads, preferred_element_type=jnp.float32
    ).astype(jnp.bfloat16)
    pick_wide = pick_rows.reshape(tok_count, top_count, feature_total)
    layer_output = jnp.sum(combine[:, :, None] * pick_wide, axis=1).astype(jnp.bfloat16)
    combine_grad = jnp.sum(upstream_wide[:, None, :] * pick_wide, axis=2)
    after_tokens = summed + 0.0 * layer_output[0, 0].astype(jnp.float32)
    gate_grad = after_tokens[:, :hidden_total][None]
    up_grad = after_tokens[:, hidden_total:][None]
    return (layer_output, token_grad, combine_grad, gate_grad, up_grad)


def solution(mesh):
    dp_size = mesh.shape["dp"]
    expert_size = mesh.shape["expert"]
    fine = Mesh(
        mesh.devices.reshape(dp_size // 4, 2, 2, 2, expert_size // 2),
        DP_AXES + EXPERT_AXES,
    )
    placed = (
        P(TOKEN_AXES, None),
        P(TOKEN_AXES, None),
        P(TOKEN_AXES, None),
        P(TOKEN_AXES, None),
        P(EXPERT_AXES, DP_AXES, None),
        P(EXPERT_AXES, DP_AXES, None),
        P(EXPERT_AXES, DP_AXES, None),
    )
    return jax.shard_map(
        shards,
        mesh=fine,
        in_specs=placed,
        out_specs=(
            P(TOKEN_AXES, None),
            P(TOKEN_AXES, None),
            P(TOKEN_AXES, None),
            P(EXPERT_AXES, DP_AXES, None),
            P(EXPERT_AXES, DP_AXES, None),
        ),
        check_vma=False,
    )
```

```python
import jax
import jax.numpy as jnp
from jax import lax
from jax.experimental.layout import Layout, with_layout_constraint
from jax.sharding import Mesh
from jax.sharding import PartitionSpec as P

DP_AXES = ("y", "xl", "c")
CHIP_AXES = ("y", "xl")
EXPERT_AXES = ("xh", "z")
TOKEN_AXES = DP_AXES + EXPERT_AXES


def expert_forward(input_rows, stacked, down_full):
    hidden_total = stacked.shape[1] // 2
    both_pre = jnp.dot(input_rows, stacked, preferred_element_type=jnp.float32)
    gate_pre = both_pre[:, :hidden_total]
    up_pre = both_pre[:, hidden_total:]
    hidden = (jax.nn.silu(gate_pre) * up_pre).astype(jnp.bfloat16)
    results = lax.dot_general(
        hidden, down_full, (((1,), (1,)), ((), ())), preferred_element_type=jnp.float32
    )
    return (results.astype(jnp.bfloat16), gate_pre, up_pre)


def expert_backward(cotangent, gate_pre, up_pre, stacked, down_full):
    hidden_grad = jnp.dot(cotangent, down_full, preferred_element_type=jnp.float32)
    sigmoid_value = jax.nn.sigmoid(gate_pre)
    gate_delta = (
        hidden_grad * up_pre * sigmoid_value * (1.0 + gate_pre * (1.0 - sigmoid_value))
    ).astype(jnp.bfloat16)
    up_delta = (hidden_grad * jax.nn.silu(gate_pre)).astype(jnp.bfloat16)
    deltas = jnp.concatenate([gate_delta, up_delta], axis=1)
    input_grads = lax.dot_general(
        deltas, stacked, (((1,), (1,)), ((), ())), preferred_element_type=jnp.float32
    )
    return (input_grads.astype(jnp.bfloat16), deltas)


def swap_partner(values, axis):
    return lax.ppermute(values, axis, perm=[(0, 1), (1, 0)])


def ring_gather(values, axis, size):
    me = lax.axis_index(axis)
    held = [values]
    moving = values
    for _ in range(size - 1):
        moving = lax.ppermute(moving, axis, perm=[(i, (i + 1) % size) for i in range(size)])
        held.append(moving)
    stacked = jnp.stack(held)
    order = (me - jnp.arange(size, dtype=jnp.int32)) % size
    return jnp.take(stacked, order, axis=0)


def ring_reduce_scatter(blocks, axis, size):
    me = lax.axis_index(axis)
    carry = lax.dynamic_index_in_dim(blocks, (me - 1) % size, axis=0, keepdims=False)
    for hop in range(size - 1):
        arrived = lax.ppermute(carry, axis, perm=[(i, (i + 1) % size) for i in range(size)])
        own = lax.dynamic_index_in_dim(blocks, (me - hop - 2) % size, axis=0, keepdims=False)
        carry = arrived + own
    return carry


def ordered_pair(own, other, axis):
    first = lax.axis_index(axis) == 0
    return jnp.stack([jnp.where(first, own, other), jnp.where(first, other, own)])


def trade_rows(buffer):
    return lax.all_to_all(buffer, EXPERT_AXES, split_axis=0, concat_axis=0, tiled=True)


def pick_slots(routing, expert_total):
    flat_ids = routing.reshape(-1)
    match_table = (flat_ids[:, None] == jnp.arange(expert_total, dtype=jnp.int32)[None, :]).astype(
        jnp.int32
    )
    position = jnp.sum((jnp.cumsum(match_table, axis=0) - 1) * match_table, axis=1)
    expert_loads = jnp.sum(match_table, axis=0)
    return (flat_ids, position, expert_loads)


def shards(tokens, routing, combine, upstream, gate_weight, up_weight, down_weight):
    tok_count = tokens.shape[0]
    top_count = routing.shape[1]
    pick_total = tok_count * top_count
    feature_total = tokens.shape[1]
    hidden_total = gate_weight.shape[2]
    expert_total = lax.axis_size(EXPERT_AXES)
    group_total = lax.axis_size(DP_AXES)
    core_total = lax.axis_size("c")
    capacity = max(tok_count // 2, top_count * tok_count // expert_total + tok_count // 4)
    local_weights = jnp.concatenate([gate_weight[0], up_weight[0], down_weight[0]], axis=1)
    y_size = lax.axis_size("y")
    along_y = ring_gather(local_weights, "y", y_size)
    along_xl = ordered_pair(along_y, swap_partner(along_y, "xl"), "xl")
    along_c = ordered_pair(along_xl, swap_partner(along_xl, "c"), "c")
    full_weights = jnp.transpose(along_c, (2, 1, 0, 3, 4)).reshape(-1, local_weights.shape[1])
    gate_full = full_weights[:, :hidden_total]
    up_full = full_weights[:, hidden_total : 2 * hidden_total]
    down_full = full_weights[:, 2 * hidden_total :]
    stacked = full_weights[:, : 2 * hidden_total]
    flat_ids, position, expert_loads = pick_slots(routing, expert_total)
    upstream_wide = upstream.astype(jnp.float32)
    pick_cotangent = (
        (combine[:, :, None] * upstream_wide[:, None, :])
        .reshape(pick_total, feature_total)
        .astype(jnp.bfloat16)
    )
    slot_index = flat_ids * capacity + position
    select = (
        slot_index[None, :] == jnp.arange(expert_total * capacity, dtype=jnp.int32)[:, None]
    ).astype(jnp.bfloat16)
    payload = jnp.concatenate([jnp.repeat(tokens, top_count, axis=0), pick_cotangent], axis=1)
    sending = jnp.dot(select, payload, preferred_element_type=jnp.float32).astype(jnp.bfloat16)
    arrived_both = trade_rows(
        sending.reshape(expert_total, capacity, 2 * feature_total)
    ).reshape(expert_total * capacity, 2 * feature_total)
    arrived = arrived_both[:, :feature_total]
    cot_arrived = arrived_both[:, feature_total:]
    results, gate_pre, up_pre = expert_forward(arrived, stacked, down_full)
    input_grads, deltas = expert_backward(cot_arrived, gate_pre, up_pre, stacked, down_full)
    piece = lax.dot_general(
        arrived, deltas, (((0,), (0,)), ((), ())), preferred_element_type=jnp.float32
    )
    slice_rows = gate_weight.shape[1]
    blocks = piece.reshape(group_total // core_total, core_total, slice_rows, 2 * hidden_total)
    core = lax.axis_index("c")
    own_blocks = lax.dynamic_index_in_dim(blocks, core, axis=1, keepdims=False)
    other_blocks = lax.dynamic_index_in_dim(blocks, 1 - core, axis=1, keepdims=False)
    core_summed = own_blocks + lax.ppermute(other_blocks, "c", perm=[(0, 1), (1, 0)])
    by_xl = core_summed.reshape(y_size, lax.axis_size("xl"), slice_rows, 2 * hidden_total)
    xl = lax.axis_index("xl")
    keep_xl = lax.dynamic_index_in_dim(by_xl, xl, axis=1, keepdims=False)
    send_xl = lax.dynamic_index_in_dim(by_xl, 1 - xl, axis=1, keepdims=False)
    xl_summed = keep_xl + swap_partner(send_xl, "xl")
    summed = ring_reduce_scatter(xl_summed, "y", y_size)
    summed = summed.reshape(slice_rows, 2 * hidden_total) / group_total
    row_major = Layout(major_to_minor=(0, 1))
    back = jnp.concatenate(
        [with_layout_constraint(results, row_major), with_layout_constraint(input_grads, row_major)],
        axis=1,
    )
    returned = trade_rows(back.reshape(expert_total, capacity, 2 * feature_total)).reshape(
        expert_total * capacity, 2 * feature_total
    )
    token_select = jnp.any(
        slot_index.reshape(tok_count, top_count)[:, :, None]
        == jnp.arange(expert_total * capacity, dtype=jnp.int32)[None, None, :],
        axis=1,
    ).astype(jnp.bfloat16)
    chooser = jnp.concatenate([select.T, token_select], axis=0)
    chosen = jnp.dot(chooser, returned, preferred_element_type=jnp.float32)
    pick_rows = chosen[:pick_total, :feature_total]
    token_grad = chosen[pick_total:, feature_total:].astype(jnp.bfloat16)
    pick_wide = pick_rows.reshape(tok_count, top_count, feature_total)
    layer_output = jnp.sum(combine[:, :, None] * pick_wide, axis=1).astype(jnp.bfloat16)
    combine_grad = jnp.sum(upstream_wide[:, None, :] * pick_wide, axis=2)
    after_tokens = summed + 0.0 * layer_output[0, 0].astype(jnp.float32)
    gate_grad = after_tokens[:, :hidden_total][None]
    up_grad = after_tokens[:, hidden_total:][None]
    return (layer_output, token_grad, combine_grad, gate_grad, up_grad)


def solution(mesh):
    dp_size = mesh.shape["dp"]
    expert_size = mesh.shape["expert"]
    fine = Mesh(
        mesh.devices.reshape(dp_size // 4, 2, 2, 2, expert_size // 2),
        DP_AXES + EXPERT_AXES,
    )
    placed = (
        P(TOKEN_AXES, None),
        P(TOKEN_AXES, None),
        P(TOKEN_AXES, None),
        P(TOKEN_AXES, None),
        P(EXPERT_AXES, DP_AXES, None),
        P(EXPERT_AXES, DP_AXES, None),
        P(EXPERT_AXES, DP_AXES, None),
    )
    return jax.shard_map(
        shards,
        mesh=fine,
        in_specs=placed,
        out_specs=(
            P(TOKEN_AXES, None),
            P(TOKEN_AXES, None),
            P(TOKEN_AXES, None),
            P(EXPERT_AXES, DP_AXES, None),
            P(EXPERT_AXES, DP_AXES, None),
        ),
        check_vma=False,
    )
```

```python
import jax
import jax.numpy as jnp
from jax import lax
from jax.experimental.layout import Layout, with_layout_constraint
from jax.sharding import Mesh
from jax.sharding import PartitionSpec as P

DP_AXES = ("y", "xl", "c")
CHIP_AXES = ("y", "xl")
EXPERT_AXES = ("xh", "z")
TOKEN_AXES = DP_AXES + EXPERT_AXES


def expert_forward(input_rows, stacked, down_full):
    hidden_total = stacked.shape[1] // 2
    both_pre = jnp.dot(input_rows, stacked, preferred_element_type=jnp.float32)
    gate_pre = both_pre[:, :hidden_total]
    up_pre = both_pre[:, hidden_total:]
    hidden = (jax.nn.silu(gate_pre) * up_pre).astype(jnp.bfloat16)
    results = lax.dot_general(
        hidden, down_full, (((1,), (1,)), ((), ())), preferred_element_type=jnp.float32
    )
    return (results.astype(jnp.bfloat16), gate_pre, up_pre)


def expert_backward(cotangent, gate_pre, up_pre, stacked, down_full):
    hidden_grad = jnp.dot(cotangent, down_full, preferred_element_type=jnp.float32)
    sigmoid_value = jax.nn.sigmoid(gate_pre)
    gate_delta = (
        hidden_grad * up_pre * sigmoid_value * (1.0 + gate_pre * (1.0 - sigmoid_value))
    ).astype(jnp.bfloat16)
    up_delta = (hidden_grad * jax.nn.silu(gate_pre)).astype(jnp.bfloat16)
    deltas = jnp.concatenate([gate_delta, up_delta], axis=1)
    input_grads = lax.dot_general(
        deltas, stacked, (((1,), (1,)), ((), ())), preferred_element_type=jnp.float32
    )
    return (input_grads.astype(jnp.bfloat16), deltas)


def swap_partner(values, axis):
    return lax.ppermute(values, axis, perm=[(0, 1), (1, 0)])


def ring_gather(values, axis, size):
    me = lax.axis_index(axis)
    held = [values]
    moving = values
    for _ in range(size - 1):
        moving = lax.ppermute(moving, axis, perm=[(i, (i + 1) % size) for i in range(size)])
        held.append(moving)
    stacked = jnp.stack(held)
    order = (me - jnp.arange(size, dtype=jnp.int32)) % size
    return jnp.take(stacked, order, axis=0)


def ring_reduce_scatter(blocks, axis, size):
    me = lax.axis_index(axis)
    carry = lax.dynamic_index_in_dim(blocks, (me - 1) % size, axis=0, keepdims=False)
    for hop in range(size - 1):
        arrived = lax.ppermute(carry, axis, perm=[(i, (i + 1) % size) for i in range(size)])
        own = lax.dynamic_index_in_dim(blocks, (me - hop - 2) % size, axis=0, keepdims=False)
        carry = arrived + own
    return carry


def ordered_pair(own, other, axis):
    first = lax.axis_index(axis) == 0
    return jnp.stack([jnp.where(first, own, other), jnp.where(first, other, own)])


def trade_rows(buffer):
    return lax.all_to_all(buffer, EXPERT_AXES, split_axis=0, concat_axis=0, tiled=True)


def pick_slots(routing, expert_total):
    flat_ids = routing.reshape(-1)
    match_table = (flat_ids[:, None] == jnp.arange(expert_total, dtype=jnp.int32)[None, :]).astype(
        jnp.int32
    )
    position = jnp.sum((jnp.cumsum(match_table, axis=0) - 1) * match_table, axis=1)
    expert_loads = jnp.sum(match_table, axis=0)
    return (flat_ids, position, expert_loads)


def shards(tokens, routing, combine, upstream, gate_weight, up_weight, down_weight):
    tok_count = tokens.shape[0]
    top_count = routing.shape[1]
    pick_total = tok_count * top_count
    feature_total = tokens.shape[1]
    hidden_total = gate_weight.shape[2]
    expert_total = lax.axis_size(EXPERT_AXES)
    group_total = lax.axis_size(DP_AXES)
    core_total = lax.axis_size("c")
    capacity = max(tok_count // 2, top_count * tok_count // expert_total + tok_count // 4)
    local_weights = jnp.concatenate([gate_weight[0], up_weight[0], down_weight[0]], axis=1)
    y_size = lax.axis_size("y")
    along_y = ring_gather(local_weights, "y", y_size)
    along_xl = ordered_pair(along_y, swap_partner(along_y, "xl"), "xl")
    along_c = ordered_pair(along_xl, swap_partner(along_xl, "c"), "c")
    full_weights = jnp.transpose(along_c, (2, 1, 0, 3, 4)).reshape(-1, local_weights.shape[1])
    gate_full = full_weights[:, :hidden_total]
    up_full = full_weights[:, hidden_total : 2 * hidden_total]
    down_full = full_weights[:, 2 * hidden_total :]
    stacked = full_weights[:, : 2 * hidden_total]
    flat_ids, position, expert_loads = pick_slots(routing, expert_total)
    upstream_wide = upstream.astype(jnp.float32)
    pick_cotangent = (
        (combine[:, :, None] * upstream_wide[:, None, :])
        .reshape(pick_total, feature_total)
        .astype(jnp.bfloat16)
    )
    slot_index = flat_ids * capacity + position
    select = (
        slot_index[None, :] == jnp.arange(expert_total * capacity, dtype=jnp.int32)[:, None]
    ).astype(jnp.bfloat16)
    payload = jnp.concatenate([jnp.repeat(tokens, top_count, axis=0), pick_cotangent], axis=1)
    sending = jnp.dot(select, payload, preferred_element_type=jnp.float32).astype(jnp.bfloat16)
    arrived_both = trade_rows(
        sending.reshape(expert_total, capacity, 2 * feature_total)
    ).reshape(expert_total * capacity, 2 * feature_total)
    arrived = arrived_both[:, :feature_total]
    cot_arrived = arrived_both[:, feature_total:]
    results, gate_pre, up_pre = expert_forward(arrived, stacked, down_full)
    input_grads, deltas = expert_backward(cot_arrived, gate_pre, up_pre, stacked, down_full)
    piece = lax.dot_general(
        arrived, deltas, (((0,), (0,)), ((), ())), preferred_element_type=jnp.float32
    )
    slice_rows = gate_weight.shape[1]
    blocks = piece.reshape(group_total // core_total, core_total, slice_rows, 2 * hidden_total)
    core = lax.axis_index("c")
    own_blocks = lax.dynamic_index_in_dim(blocks, core, axis=1, keepdims=False)
    other_blocks = lax.dynamic_index_in_dim(blocks, 1 - core, axis=1, keepdims=False)
    core_summed = own_blocks + lax.ppermute(other_blocks, "c", perm=[(0, 1), (1, 0)])
    by_xl = core_summed.reshape(y_size, lax.axis_size("xl"), slice_rows, 2 * hidden_total)
    xl = lax.axis_index("xl")
    keep_xl = lax.dynamic_index_in_dim(by_xl, xl, axis=1, keepdims=False)
    send_xl = lax.dynamic_index_in_dim(by_xl, 1 - xl, axis=1, keepdims=False)
    xl_summed = keep_xl + swap_partner(send_xl, "xl")
    summed = ring_reduce_scatter(xl_summed, "y", y_size)
    summed = summed.reshape(slice_rows, 2 * hidden_total) / group_total
    row_major = Layout(major_to_minor=(0, 1))
    back = jnp.concatenate(
        [with_layout_constraint(results, row_major), with_layout_constraint(input_grads, row_major)],
        axis=1,
    )
    returned = trade_rows(back.reshape(expert_total, capacity, 2 * feature_total)).reshape(
        expert_total * capacity, 2 * feature_total
    )
    pick_rows = lax.dot_general(
        select,
        returned[:, :feature_total],
        (((0,), (0,)), ((), ())),
        preferred_element_type=jnp.float32,
    )
    token_select = jnp.any(
        slot_index.reshape(tok_count, top_count)[:, :, None]
        == jnp.arange(expert_total * capacity, dtype=jnp.int32)[None, None, :],
        axis=1,
    ).astype(jnp.bfloat16)
    token_grad = jnp.dot(
        token_select, returned[:, feature_total:], preferred_element_type=jnp.float32
    ).astype(jnp.bfloat16)
    pick_wide = pick_rows.reshape(tok_count, top_count, feature_total)
    layer_output = jnp.sum(combine[:, :, None] * pick_wide, axis=1).astype(jnp.bfloat16)
    combine_grad = jnp.sum(upstream_wide[:, None, :] * pick_wide, axis=2)
    after_tokens = summed
    gate_grad = after_tokens[:, :hidden_total][None]
    up_grad = after_tokens[:, hidden_total:][None]
    return (layer_output, token_grad, combine_grad, gate_grad, up_grad)


def solution(mesh):
    dp_size = mesh.shape["dp"]
    expert_size = mesh.shape["expert"]
    fine = Mesh(
        mesh.devices.reshape(dp_size // 4, 2, 2, 2, expert_size // 2),
        DP_AXES + EXPERT_AXES,
    )
    placed = (
        P(TOKEN_AXES, None),
        P(TOKEN_AXES, None),
        P(TOKEN_AXES, None),
        P(TOKEN_AXES, None),
        P(EXPERT_AXES, DP_AXES, None),
        P(EXPERT_AXES, DP_AXES, None),
        P(EXPERT_AXES, DP_AXES, None),
    )
    return jax.shard_map(
        shards,
        mesh=fine,
        in_specs=placed,
        out_specs=(
            P(TOKEN_AXES, None),
            P(TOKEN_AXES, None),
            P(TOKEN_AXES, None),
            P(EXPERT_AXES, DP_AXES, None),
            P(EXPERT_AXES, DP_AXES, None),
        ),
        check_vma=False,
    )
```
